256 devices in a mesh: dp: 32 (over x_lo, z, core), tensor: 8 (over x_hi, y).
Axes of the slice: x: 4 (x_hi: 2, x_lo: 2; x = x_hi * 2 + x_lo), y: 4, z: 8, core: 2. Of those that a mesh axis runs over, the one named last changes fastest.
Arguments:
- hidden_input_state: bfloat16 [12288, 4608], P('dp', 'tensor'), may hold values from -80 to 80
- norm_gain: float32 [4608], replicated, may hold values from 0.5 to 1.5
- head_weight: bfloat16 [4608, 8192], P(None, 'tensor'), may hold values from -2 to 2
- target_ids: int32 [12288], P('dp'), may hold values from 0 to 8191
Outputs:
- hidden_state_gradient: float32 [12288, 4608], P('dp', 'tensor')
- grad_head: float32 [4608, 8192], P('dp', 'tensor')
- norm_gain_gradient: float32 [4608], P('tensor')
The draws below stay inside these ranges and needn't reach their ends.
All inputs are finite; a program needn't handle non-finite values.
Results may differ from the reference program's by a relative error of at most 0.0039.
Values may be sent and summed in bfloat16 or wider, within the bound.
No kernel may reach another device: no remote copies, remote signals or barrier semaphores. Data moves between devices by JAX's collectives and lax.ppermute only.
A program may use at most 192 MiB of HBM per device.

```python
import math
import jax
import jax.numpy as jnp
from jax import lax

D = 4608
VOCAB = 8192
TOKENS = 12288


strength_table = (120.0, 160.0, 200.0, 240.0)


def directions(key):
    return jnp.clip(jax.random.normal(jax.random.fold_in(key, 7), (4, D), jnp.float32), -5.0, 5.0)


def common_row(key):
    return jnp.clip(jax.random.normal(jax.random.fold_in(key, 23), (1, D), jnp.float32), -5.0, 5.0)


def draw_head_weight(key, part):
    base = jnp.clip(jax.random.normal(jax.random.fold_in(key, 11), (D, VOCAB), jnp.float32), -5.0, 5.0)
    position = jnp.arange(VOCAB).astype(jnp.float32) / VOCAB
    spread = jax.random.uniform(jax.random.fold_in(key, 12), (VOCAB,), jnp.float32, 0.0, math.log(3.4))
    scale = 0.1 * jnp.exp(math.log(3.0) * position + spread) / math.sqrt(D)
    drawn = base * scale[None, :]
    unit = directions(key)
    which = jnp.arange(VOCAB) - (VOCAB - 8)
    hot = which >= 0
    clipped = jnp.clip(which, 0, 7)
    group = clipped // 2
    strength = jnp.array(strength_table, jnp.float32)[group] + 2.0 * (clipped % 2).astype(jnp.float32)
    aligned = unit[group].T * (strength / D)[None, :] + 0.05 * drawn
    return jnp.where(hot[None, :], aligned, drawn).astype(jnp.bfloat16)


def draw_hidden_input_state(key, part):
    noise = jnp.clip(jax.random.normal(jax.random.fold_in(key, 21), (TOKENS, D), jnp.float32), -5.0, 5.0)
    common = common_row(key)
    return (noise + 0.7 * common).astype(jnp.bfloat16)


def place_ends(entries, rng, low, top_value):
    index_at = [jax.random.randint(jax.random.fold_in(rng, axis), (), 0, length) for axis, length in enumerate(entries.shape)]
    main_axis = entries.shape.index(max(entries.shape))
    beside = index_at[:main_axis] + [(index_at[main_axis] + 1) % entries.shape[main_axis]] + index_at[main_axis + 1:]
    return entries.at[tuple(index_at)].set(low).at[tuple(beside)].set(top_value)


def setup_inputs(seed: int = 0) -> dict:
    seeds = jax.random.split(jax.random.key(seed), 5)
    hidden_input_state = draw_hidden_input_state(jax.random.fold_in(seeds[4], 71), 0)
    norm_gain = jnp.clip(1.0 + 0.1 * jax.random.normal(seeds[1], (D,), jnp.float32), 0.5, 1.5)
    head_weight = draw_head_weight(jax.random.fold_in(seeds[4], 71), 0)
    target_ids = place_ends(jax.random.randint(seeds[3], (TOKENS,), 0, VOCAB), jax.random.fold_in(seeds[3], 1), 0, VOCAB - 1).astype(jnp.int32)
    return {"hidden_input_state": hidden_input_state, "norm_gain": norm_gain, "head_weight": head_weight, "target_ids": target_ids}


epsilon = 1e-06

def reference(hidden_input_state, norm_gain, head_weight, target_ids):
    token_blocks = 8
    gain_row = norm_gain.astype(jnp.float32)
    blocked = hidden_input_state.reshape(token_blocks, -1, D)
    target_blocks = target_ids.reshape(token_blocks, -1)
    column_ids = lax.broadcasted_iota(jnp.int32, (1, VOCAB), 1)

    def one_block(carry, inputs):
        head_total, gain_total = carry
        block_rows, block_targets = inputs
        values = block_rows.astype(jnp.float32)
        scaled_rows = lax.rsqrt(lax.optimization_barrier(jnp.mean(values * values, axis=1, keepdims=True)) + epsilon)
        normalized = values * scaled_rows
        normed = (normalized * gain_row[None, :]).astype(jnp.bfloat16)
        logits = jnp.dot(normed, head_weight, preferred_element_type=jnp.float32)
        row_top = lax.optimization_barrier(jnp.max(logits, axis=1, keepdims=True))
        log_total = row_top + jnp.log(lax.optimization_barrier(jnp.sum(jnp.exp(logits - row_top), axis=1, keepdims=True)))
        onehot = (column_ids == block_targets.astype(jnp.int32)[:, None]).astype(jnp.float32)
        dlogits = (jnp.exp(logits - log_total) - onehot).astype(jnp.bfloat16)
        normed_gradient = lax.dot_general(dlogits, head_weight, (((1,), (1,)), ((), ())), preferred_element_type=jnp.float32)
        weighted_rows = normed_gradient * gain_row[None, :]
        row_inner_sum = lax.optimization_barrier(jnp.mean(weighted_rows * normalized, axis=1, keepdims=True))
        grad_rows = scaled_rows * (weighted_rows - normalized * row_inner_sum)
        head_total = head_total + lax.dot_general(normed, dlogits, (((0,), (0,)), ((), ())), preferred_element_type=jnp.float32)
        gain_total = gain_total + lax.optimization_barrier(jnp.sum(normed_gradient * normalized, axis=0))
        return ((head_total, gain_total), grad_rows)
    start_carry = (jnp.zeros((D, VOCAB), jnp.float32), jnp.zeros((D,), jnp.float32))
    (grad_head, norm_gain_gradient), grad_blocks = lax.scan(one_block, start_carry, (blocked, target_blocks))
    return (grad_blocks.reshape(TOKENS, D), grad_head, norm_gain_gradient)
```

```python
import jax
import jax.numpy as jnp
import numpy as np
from jax import lax
from jax.sharding import PartitionSpec as P

epsilon = 1e-06


def ring_order(n_hi, n_lo):
    order = []
    for hi in range(n_hi):
        los = range(n_lo) if hi % 2 == 0 else range(n_lo - 1, -1, -1)
        order += [hi * n_lo + lo for lo in los]
    return order


def ring_reduce_scatter(fwd, bwd, axis, order):
    n = len(order)
    pos_of = np.zeros(n, np.int32)
    for p, t in enumerate(order):
        pos_of[t] = p
    order_arr = jnp.asarray(np.asarray(order, np.int32))
    me = lax.axis_index(axis)
    pos = jnp.asarray(pos_of)[me]
    perm_f = [(order[p], order[(p + 1) % n]) for p in range(n)]
    perm_b = [(order[p], order[(p - 1) % n]) for p in range(n)]
    recv_f = recv_b = None
    for s in range(n - 1):
        qf = order_arr[(pos - 1 - s) % n]
        qb = order_arr[(pos + 1 + s) % n]
        send_f = lax.dynamic_index_in_dim(fwd, qf, 0, keepdims=False)
        send_b = lax.dynamic_index_in_dim(bwd, qb, 0, keepdims=False)
        if recv_f is not None:
            send_f = send_f + recv_f
            send_b = send_b + recv_b
        recv_f = lax.ppermute(send_f, axis, perm_f)
        recv_b = lax.ppermute(send_b, axis, perm_b)
    own_f = lax.dynamic_index_in_dim(fwd, me, 0, keepdims=False)
    own_b = lax.dynamic_index_in_dim(bwd, me, 0, keepdims=False)
    return own_f + recv_f, own_b + recv_b


def shards(hidden_input_state, norm_gain, head_weight, target_ids):
    tokens, local_cols = hidden_input_state.shape
    width, vocab_rows = head_weight.shape
    n_tensor = width // local_cols
    gathered = lax.all_gather(hidden_input_state, "tensor", axis=1, tiled=True)
    values = gathered.astype(jnp.float32)
    scaled_rows = lax.rsqrt(jnp.mean(values * values, axis=1, keepdims=True) + epsilon)
    normalized = values * scaled_rows
    normed = (normalized * norm_gain[None, :]).astype(jnp.bfloat16)
    logits = jnp.dot(normed, head_weight, preferred_element_type=jnp.float32)
    local_top = jnp.max(logits, axis=1)
    local_total = jnp.sum(jnp.exp(logits - local_top[:, None]), axis=1)
    stats = lax.all_gather(jnp.stack([local_top, local_total]), "tensor", axis=0)
    row_top = jnp.max(stats[:, 0, :], axis=0)
    row_total = jnp.sum(stats[:, 1, :] * jnp.exp(stats[:, 0, :] - row_top[None, :]), axis=0)
    log_total = row_top + jnp.log(row_total)
    offset = lax.axis_index("tensor") * vocab_rows
    column_ids = offset + lax.broadcasted_iota(jnp.int32, (1, vocab_rows), 1)
    onehot = (column_ids == target_ids[:, None]).astype(jnp.float32)
    dlogits = (jnp.exp(logits - log_total[:, None]) - onehot).astype(jnp.bfloat16)

    grad_head = lax.psum_scatter(
        lax.dot_general(
            normed, dlogits, (((0,), (0,)), ((), ())), preferred_element_type=jnp.float32
        ),
        "dp",
        scatter_dimension=0,
        tiled=True,
    )

    partial = lax.dot_general(
        head_weight, dlogits, (((1,), (1,)), ((), ())), preferred_element_type=jnp.float32
    )
    inner_part = jnp.sum(partial * (norm_gain[:, None] * normalized.T), axis=0)
    chunks = partial.reshape(n_tensor, local_cols, tokens)
    half = local_cols // 2
    extra = jnp.zeros((n_tensor, 8, tokens), jnp.float32).at[:, 0, :].set(
        jnp.broadcast_to(inner_part[None, :], (n_tensor, tokens))
    )
    fwd = jnp.concatenate([chunks[:, :half, :], extra], axis=1)
    bwd = chunks[:, half:, :]
    order = ring_order(2, n_tensor // 2)
    got_f, got_b = ring_reduce_scatter(fwd, bwd, "tensor", order)
    grad_cols = jnp.concatenate([got_f[:half], got_b], axis=0)
    row_inner_sum = got_f[half] / width

    normed_gradient = grad_cols.T
    start_col = lax.axis_index("tensor") * local_cols
    normalized_slice = hidden_input_state.astype(jnp.float32) * scaled_rows
    gain_slice = lax.dynamic_slice_in_dim(norm_gain, start_col, local_cols)
    weighted_rows = normed_gradient * gain_slice[None, :]
    hidden_state_gradient = scaled_rows * (
        weighted_rows - normalized_slice * row_inner_sum[:, None]
    )
    norm_gain_gradient = lax.psum(jnp.sum(normed_gradient * normalized_slice, axis=0), "dp")
    return (hidden_state_gradient, grad_head, norm_gain_gradient)


def solution(mesh):
    return jax.shard_map(
        shards,
        mesh=mesh,
        in_specs=(P("dp", "tensor"), P(), P(None, "tensor"), P("dp")),
        out_specs=(P("dp", "tensor"), P("dp", "tensor"), P("tensor")),
        check_vma=False,
    )
```

```python
import jax
import jax.numpy as jnp
from jax import lax
from jax.sharding import PartitionSpec as P

epsilon = 1e-06


def shift_gather(x, axis, n):
    me = lax.axis_index(axis)
    got = [x]
    for k in range(1, n):
        got.append(lax.ppermute(x, axis, [(c, (c + k) % n) for c in range(n)]))
    rev = jnp.stack(got[::-1])
    doubled = jnp.concatenate([rev, rev], axis=0)
    return lax.dynamic_slice_in_dim(doubled, (n - 1) - me, n, axis=0)


def butterfly_sum(x, axis, n):
    b = 1
    while b < n:
        x = x + lax.ppermute(x, axis, [(c, c ^ b) for c in range(n)])
        b *= 2
    return x


def two_stage_reduce_scatter(parts, axis, n_hi, n_lo):
    me = lax.axis_index(axis)
    h = me // n_lo
    lo = me % n_lo
    rows = parts.shape[2]
    half = rows // 2
    fwd = parts[:, :, :half, :]
    bwd = parts[:, :, half:, :]
    perm_f = [(a * n_lo + l, a * n_lo + (l + 1) % n_lo) for a in range(n_hi) for l in range(n_lo)]
    perm_b = [(a * n_lo + l, a * n_lo + (l - 1) % n_lo) for a in range(n_hi) for l in range(n_lo)]
    recv_f = recv_b = None
    for s in range(n_lo - 1):
        send_f = lax.dynamic_index_in_dim(fwd, (lo - 1 - s) % n_lo, 1, keepdims=False)
        send_b = lax.dynamic_index_in_dim(bwd, (lo + 1 + s) % n_lo, 1, keepdims=False)
        if recv_f is not None:
            send_f = send_f + recv_f
            send_b = send_b + recv_b
        recv_f = lax.ppermute(send_f, axis, perm_f)
        recv_b = lax.ppermute(send_b, axis, perm_b)
    sum_f = lax.dynamic_index_in_dim(fwd, lo, 1, keepdims=False) + recv_f
    sum_b = lax.dynamic_index_in_dim(bwd, lo, 1, keepdims=False) + recv_b
    perm_h = [(a * n_lo + l, (n_hi - 1 - a) * n_lo + l) for a in range(n_hi) for l in range(n_lo)]
    out_f = lax.dynamic_index_in_dim(sum_f, h, 0, keepdims=False) + lax.ppermute(
        lax.dynamic_index_in_dim(sum_f, n_hi - 1 - h, 0, keepdims=False), axis, perm_h
    )
    out_b = lax.dynamic_index_in_dim(sum_b, h, 0, keepdims=False) + lax.ppermute(
        lax.dynamic_index_in_dim(sum_b, n_hi - 1 - h, 0, keepdims=False), axis, perm_h
    )
    return jnp.concatenate([out_f, out_b], axis=0)


def shards(hidden_input_state, norm_gain, head_weight, target_ids):
    tokens, local_cols = hidden_input_state.shape
    width, vocab_rows = head_weight.shape
    n_tensor = width // local_cols
    n_dp = lax.psum(1, "dp")
    blocks = shift_gather(hidden_input_state, "tensor", n_tensor)
    gathered = jnp.transpose(blocks, (1, 0, 2)).reshape(tokens, width)
    values = gathered.astype(jnp.float32)
    scaled_rows = lax.rsqrt(jnp.mean(values * values, axis=1, keepdims=True) + epsilon)
    normalized = values * scaled_rows
    normed = (normalized * norm_gain[None, :]).astype(jnp.bfloat16)
    logits = jnp.dot(normed, head_weight, preferred_element_type=jnp.float32)
    local_top = jnp.max(logits, axis=1)
    local_total = jnp.sum(jnp.exp(logits - local_top[:, None]), axis=1)
    stats = shift_gather(jnp.stack([local_top, local_total]), "tensor", n_tensor)
    row_top = jnp.max(stats[:, 0, :], axis=0)
    row_total = jnp.sum(stats[:, 1, :] * jnp.exp(stats[:, 0, :] - row_top[None, :]), axis=0)
    log_total = row_top + jnp.log(row_total)
    offset = lax.axis_index("tensor") * vocab_rows
    column_ids = offset + lax.broadcasted_iota(jnp.int32, (1, vocab_rows), 1)
    onehot = (column_ids == target_ids[:, None]).astype(jnp.float32)
    dlogits = (jnp.exp(logits - log_total[:, None]) - onehot).astype(jnp.bfloat16)

    grad_head = lax.psum_scatter(
        lax.dot_general(
            normed, dlogits, (((0,), (0,)), ((), ())), preferred_element_type=jnp.float32
        ),
        "dp",
        scatter_dimension=0,
        tiled=True,
    )

    partial = lax.dot_general(
        head_weight, dlogits, (((1,), (1,)), ((), ())), preferred_element_type=jnp.float32
    )
    normalized_t = normalized.T
    inner_part = jnp.sum(partial * (norm_gain[:, None] * normalized_t), axis=0)
    gain_part = jnp.sum(partial * normalized_t, axis=1)

    n_lo = 4 if n_tensor % 4 == 0 else n_tensor
    n_hi = n_tensor // n_lo
    grad_cols = two_stage_reduce_scatter(
        partial.reshape(n_hi, n_lo, local_cols, tokens), "tensor", n_hi, n_lo
    )
    row_inner_sum = jnp.sum(shift_gather(inner_part, "tensor", n_tensor), axis=0) / width

    normed_gradient = grad_cols.T
    start_col = lax.axis_index("tensor") * local_cols
    normalized_slice = hidden_input_state.astype(jnp.float32) * scaled_rows
    gain_slice = lax.dynamic_slice_in_dim(norm_gain, start_col, local_cols)
    weighted_rows = normed_gradient * gain_slice[None, :]
    hidden_state_gradient = scaled_rows * (
        weighted_rows - normalized_slice * row_inner_sum[:, None]
    )
    gain_total = butterfly_sum(butterfly_sum(gain_part, "dp", n_dp), "tensor", n_tensor)
    norm_gain_gradient = lax.dynamic_slice_in_dim(gain_total, start_col, local_cols)
    return (hidden_state_gradient, grad_head, norm_gain_gradient)


def solution(mesh):
    return jax.shard_map(
        shards,
        mesh=mesh,
        in_specs=(P("dp", "tensor"), P(), P(None, "tensor"), P("dp")),
        out_specs=(P("dp", "tensor"), P("dp", "tensor"), P("tensor")),
        check_vma=False,
    )
```

```python
import jax
import jax.numpy as jnp
from jax import lax
from jax.sharding import Mesh, PartitionSpec as P

epsilon = 1e-06


def shift_gather(x, axis, n):
    me = lax.axis_index(axis)
    got = [x]
    for k in range(1, n):
        got.append(lax.ppermute(x, axis, [(c, (c + k) % n) for c in range(n)]))
    rev = jnp.stack(got[::-1])
    doubled = jnp.concatenate([rev, rev], axis=0)
    return lax.dynamic_slice_in_dim(doubled, (n - 1) - me, n, axis=0)


def butterfly_sum(x, axis, n):
    b = 1
    while b < n:
        x = x + lax.ppermute(x, axis, [(c, c ^ b) for c in range(n)])
        b *= 2
    return x


def two_stage_reduce_scatter(parts, axis, n_hi, n_lo):
    me = lax.axis_index(axis)
    h = me // n_lo
    lo = me % n_lo
    rows = parts.shape[2]
    half = (rows // 2) // 8 * 8
    fwd = parts[:, :, :half, :]
    bwd = parts[:, :, half:, :]
    perm_f = [(a * n_lo + l, a * n_lo + (l + 1) % n_lo) for a in range(n_hi) for l in range(n_lo)]
    perm_b = [(a * n_lo + l, a * n_lo + (l - 1) % n_lo) for a in range(n_hi) for l in range(n_lo)]
    recv_f = recv_b = None
    for s in range(n_lo - 1):
        send_f = lax.dynamic_index_in_dim(fwd, (lo - 1 - s) % n_lo, 1, keepdims=False)
        send_b = lax.dynamic_index_in_dim(bwd, (lo + 1 + s) % n_lo, 1, keepdims=False)
        if recv_f is not None:
            send_f = send_f + recv_f
            send_b = send_b + recv_b
        recv_f = lax.ppermute(send_f, axis, perm_f)
        recv_b = lax.ppermute(send_b, axis, perm_b)
    sum_f = lax.dynamic_index_in_dim(fwd, lo, 1, keepdims=False) + recv_f
    sum_b = lax.dynamic_index_in_dim(bwd, lo, 1, keepdims=False) + recv_b
    perm_h = [(a * n_lo + l, (n_hi - 1 - a) * n_lo + l) for a in range(n_hi) for l in range(n_lo)]
    out_f = lax.dynamic_index_in_dim(sum_f, h, 0, keepdims=False) + lax.ppermute(
        lax.dynamic_index_in_dim(sum_f, n_hi - 1 - h, 0, keepdims=False), axis, perm_h
    )
    out_b = lax.dynamic_index_in_dim(sum_b, h, 0, keepdims=False) + lax.ppermute(
        lax.dynamic_index_in_dim(sum_b, n_hi - 1 - h, 0, keepdims=False), axis, perm_h
    )
    return jnp.concatenate([out_f, out_b], axis=0)


def shards(hidden_input_state, norm_gain, head_weight, target_ids):
    tokens, local_cols = hidden_input_state.shape
    width, vocab_rows = head_weight.shape
    n_tensor = width // local_cols
    n_outer = lax.psum(1, "outer")
    blocks = shift_gather(hidden_input_state, "tensor", n_tensor)
    gathered = jnp.transpose(blocks, (1, 0, 2)).reshape(tokens, width)
    values = gathered.astype(jnp.float32)
    scaled_rows = lax.rsqrt(jnp.mean(values * values, axis=1, keepdims=True) + epsilon)
    normalized = values * scaled_rows
    normed = (normalized * norm_gain[None, :]).astype(jnp.bfloat16)
    logits = jnp.dot(normed, head_weight, preferred_element_type=jnp.float32)
    local_top = jnp.max(logits, axis=1)
    local_total = jnp.sum(jnp.exp(logits - local_top[:, None]), axis=1)
    stats = shift_gather(jnp.stack([local_top, local_total]), "tensor", n_tensor)
    row_top = jnp.max(stats[:, 0, :], axis=0)
    row_total = jnp.sum(stats[:, 1, :] * jnp.exp(stats[:, 0, :] - row_top[None, :]), axis=0)
    log_total = row_top + jnp.log(row_total)
    offset = lax.axis_index("tensor") * vocab_rows
    column_ids = offset + lax.broadcasted_iota(jnp.int32, (1, vocab_rows), 1)
    onehot = (column_ids == target_ids[:, None]).astype(jnp.float32)
    dlogits = (jnp.exp(logits - log_total[:, None]) - onehot).astype(jnp.bfloat16)

    head_partial = lax.dot_general(
        normed, dlogits, (((0,), (0,)), ((), ())), preferred_element_type=jnp.float32
    )
    core = lax.axis_index("core")
    by_core = head_partial.reshape(n_outer, 2, width // (2 * n_outer), vocab_rows)
    sent = lax.ppermute(
        lax.dynamic_index_in_dim(by_core, 1 - core, 1, keepdims=False), "core", [(0, 1), (1, 0)]
    )
    kept = lax.dynamic_index_in_dim(by_core, core, 1, keepdims=False) + sent
    grad_head = lax.psum_scatter(
        kept.reshape(width // 2, vocab_rows), "outer", scatter_dimension=0, tiled=True
    )

    partial = lax.dot_general(
        head_weight, dlogits, (((1,), (1,)), ((), ())), preferred_element_type=jnp.float32
    )
    normalized_t = normalized.T
    inner_part = jnp.sum(partial * (norm_gain[:, None] * normalized_t), axis=0)
    gain_part = jnp.sum(partial * normalized_t, axis=1)

    n_lo = 4 if n_tensor % 4 == 0 else n_tensor
    n_hi = n_tensor // n_lo
    gain_rows = -(-local_cols // tokens)
    gain_chunks = jnp.pad(
        gain_part.reshape(n_tensor, local_cols), ((0, 0), (0, gain_rows * tokens - local_cols))
    ).reshape(n_tensor, gain_rows, tokens)
    extra = jnp.concatenate(
        [
            jnp.broadcast_to(inner_part[None, None, :], (n_tensor, 1, tokens)),
            gain_chunks,
            jnp.zeros((n_tensor, 7 - gain_rows, tokens), jnp.float32),
        ],
        axis=1,
    )
    chunks = jnp.concatenate([partial.reshape(n_tensor, local_cols, tokens), extra], axis=1)
    summed = two_stage_reduce_scatter(
        chunks.reshape(n_hi, n_lo, local_cols + 8, tokens), "tensor", n_hi, n_lo
    )
    grad_cols = summed[:local_cols]
    row_inner_sum = summed[local_cols] / width
    gain_local = summed[local_cols + 1 : local_cols + 1 + gain_rows].reshape(-1)[:local_cols]

    normed_gradient = grad_cols.T
    start_col = lax.axis_index("tensor") * local_cols
    normalized_slice = hidden_input_state.astype(jnp.float32) * scaled_rows
    gain_slice = lax.dynamic_slice_in_dim(norm_gain, start_col, local_cols)
    weighted_rows = normed_gradient * gain_slice[None, :]
    hidden_state_gradient = scaled_rows * (
        weighted_rows - normalized_slice * row_inner_sum[:, None]
    )
    norm_gain_gradient = butterfly_sum(butterfly_sum(gain_local, "outer", n_outer), "core", 2)
    return (hidden_state_gradient, grad_head, norm_gain_gradient)


def solution(mesh):
    n_dp, n_tensor = mesh.devices.shape
    split = Mesh(mesh.devices.reshape(n_dp // 2, 2, n_tensor), ("outer", "core", "tensor"))
    dp = ("outer", "core")
    return jax.shard_map(
        shards,
        mesh=split,
        in_specs=(P(dp, "tensor"), P(), P(None, "tensor"), P(dp)),
        out_specs=(P(dp, "tensor"), P(dp, "tensor"), P("tensor")),
        check_vma=False,
    )
```

```python
import jax
import jax.numpy as jnp
from jax import lax
from jax.sharding import Mesh, PartitionSpec as P

epsilon = 1e-06


def shift_gather(x, axis, n):
    me = lax.axis_index(axis)
    got = [x]
    for k in range(1, n):
        got.append(lax.ppermute(x, axis, [(c, (c + k) % n) for c in range(n)]))
    rev = jnp.stack(got[::-1])
    doubled = jnp.concatenate([rev, rev], axis=0)
    return lax.dynamic_slice_in_dim(doubled, (n - 1) - me, n, axis=0)


def butterfly_sum(x, axis, n):
    b = 1
    while b < n:
        x = x + lax.ppermute(x, axis, [(c, c ^ b) for c in range(n)])
        b *= 2
    return x


def two_stage_reduce_scatter(parts, axis, n_hi, n_lo):
    me = lax.axis_index(axis)
    h = me // n_lo
    lo = me % n_lo
    rows = parts.shape[2]
    half = (rows // 2) // 8 * 8
    fwd = parts[:, :, :half, :]
    bwd = parts[:, :, half:, :]
    perm_f = [(a * n_lo + l, a * n_lo + (l + 1) % n_lo) for a in range(n_hi) for l in range(n_lo)]
    perm_b = [(a * n_lo + l, a * n_lo + (l - 1) % n_lo) for a in range(n_hi) for l in range(n_lo)]
    recv_f = recv_b = None
    for s in range(n_lo - 1):
        send_f = lax.dynamic_index_in_dim(fwd, (lo - 1 - s) % n_lo, 1, keepdims=False)
        send_b = lax.dynamic_index_in_dim(bwd, (lo + 1 + s) % n_lo, 1, keepdims=False)
        if recv_f is not None:
            send_f = send_f + recv_f
            send_b = send_b + recv_b
        recv_f = lax.ppermute(send_f, axis, perm_f)
        recv_b = lax.ppermute(send_b, axis, perm_b)
    sum_f = lax.dynamic_index_in_dim(fwd, lo, 1, keepdims=False) + recv_f
    sum_b = lax.dynamic_index_in_dim(bwd, lo, 1, keepdims=False) + recv_b
    perm_h = [(a * n_lo + l, (n_hi - 1 - a) * n_lo + l) for a in range(n_hi) for l in range(n_lo)]
    out_f = lax.dynamic_index_in_dim(sum_f, h, 0, keepdims=False) + lax.ppermute(
        lax.dynamic_index_in_dim(sum_f, n_hi - 1 - h, 0, keepdims=False), axis, perm_h
    )
    out_b = lax.dynamic_index_in_dim(sum_b, h, 0, keepdims=False) + lax.ppermute(
        lax.dynamic_index_in_dim(sum_b, n_hi - 1 - h, 0, keepdims=False), axis, perm_h
    )
    return jnp.concatenate([out_f, out_b], axis=0)


def shards(hidden_input_state, norm_gain, head_weight, target_ids):
    tokens, local_cols = hidden_input_state.shape
    width, vocab_rows = head_weight.shape
    n_tensor = width // local_cols
    n_outer = lax.psum(1, "outer")
    blocks = shift_gather(hidden_input_state, "tensor", n_tensor)
    gathered = jnp.transpose(blocks, (1, 0, 2)).reshape(tokens, width)
    values = gathered.astype(jnp.float32)
    scaled_rows = lax.rsqrt(jnp.mean(values * values, axis=1, keepdims=True) + epsilon)
    normalized = values * scaled_rows
    normed = (normalized * norm_gain[None, :]).astype(jnp.bfloat16)
    logits = jnp.dot(normed, head_weight, preferred_element_type=jnp.float32)
    local_top = jnp.max(logits, axis=1)
    local_total = jnp.sum(jnp.exp(logits - local_top[:, None]), axis=1)
    stats = shift_gather(jnp.stack([local_top, local_total]), "tensor", n_tensor)
    row_top = jnp.max(stats[:, 0, :], axis=0)
    row_total = jnp.sum(stats[:, 1, :] * jnp.exp(stats[:, 0, :] - row_top[None, :]), axis=0)
    log_total = row_top + jnp.log(row_total)
    offset = lax.axis_index("tensor") * vocab_rows
    column_ids = offset + lax.broadcasted_iota(jnp.int32, (1, vocab_rows), 1)
    onehot = (column_ids == target_ids[:, None]).astype(jnp.float32)
    dlogits = (jnp.exp(logits - log_total[:, None]) - onehot).astype(jnp.bfloat16)

    head_partial = lax.dot_general(
        normed, dlogits, (((0,), (0,)), ((), ())), preferred_element_type=jnp.float32
    )
    grad_head = lax.psum_scatter(head_partial, ("outer", "core"), scatter_dimension=0, tiled=True)

    partial = lax.dot_general(
        head_weight, dlogits, (((1,), (1,)), ((), ())), preferred_element_type=jnp.float32
    )
    normalized_t = normalized.T
    inner_part = jnp.sum(partial * (norm_gain[:, None] * normalized_t), axis=0)
    gain_part = jnp.sum(partial * normalized_t, axis=1)

    n_lo = 4 if n_tensor % 4 == 0 else n_tensor
    n_hi = n_tensor // n_lo
    gain_rows = -(-local_cols // tokens)
    gain_chunks = jnp.pad(
        gain_part.reshape(n_tensor, local_cols), ((0, 0), (0, gain_rows * tokens - local_cols))
    ).reshape(n_tensor, gain_rows, tokens)
    extra = jnp.concatenate(
        [
            jnp.broadcast_to(inner_part[None, None, :], (n_tensor, 1, tokens)),
            gain_chunks,
            jnp.zeros((n_tensor, 7 - gain_rows, tokens), jnp.float32),
        ],
        axis=1,
    )
    chunks = jnp.concatenate([partial.reshape(n_tensor, local_cols, tokens), extra], axis=1)
    summed = two_stage_reduce_scatter(
        chunks.reshape(n_hi, n_lo, local_cols + 8, tokens), "tensor", n_hi, n_lo
    )
    grad_cols = summed[:local_cols]
    row_inner_sum = summed[local_cols] / width
    gain_local = summed[local_cols + 1 : local_cols + 1 + gain_rows].reshape(-1)[:local_cols]

    normed_gradient = grad_cols.T
    start_col = lax.axis_index("tensor") * local_cols
    normalized_slice = hidden_input_state.astype(jnp.float32) * scaled_rows
    gain_slice = lax.dynamic_slice_in_dim(norm_gain, start_col, local_cols)
    weighted_rows = normed_gradient * gain_slice[None, :]
    hidden_state_gradient = scaled_rows * (
        weighted_rows - normalized_slice * row_inner_sum[:, None]
    )
    norm_gain_gradient = butterfly_sum(butterfly_sum(gain_local, "outer", n_outer), "core", 2)
    return (hidden_state_gradient, grad_head, norm_gain_gradient)


def solution(mesh):
    n_dp, n_tensor = mesh.devices.shape
    split = Mesh(mesh.devices.reshape(n_dp // 2, 2, n_tensor), ("outer", "core", "tensor"))
    dp = ("outer", "core")
    return jax.shard_map(
        shards,
        mesh=split,
        in_specs=(P(dp, "tensor"), P(), P(None, "tensor"), P(dp)),
        out_specs=(P(dp, "tensor"), P(dp, "tensor"), P("tensor")),
        check_vma=False,
    )
```

```python
import jax
import jax.numpy as jnp
from jax import lax
from jax.sharding import Mesh, PartitionSpec as P

epsilon = 1e-06


def shift_gather(x, axis, n):
    me = lax.axis_index(axis)
    got = [x]
    for k in range(1, n):
        got.append(lax.ppermute(x, axis, [(c, (c + k) % n) for c in range(n)]))
    rev = jnp.stack(got[::-1])
    doubled = jnp.concatenate([rev, rev], axis=0)
    return lax.dynamic_slice_in_dim(doubled, (n - 1) - me, n, axis=0)


def butterfly_sum(x, axis, n):
    b = 1
    while b < n:
        x = x + lax.ppermute(x, axis, [(c, c ^ b) for c in range(n)])
        b *= 2
    return x


def butterfly_softmax_stats(top, logits, axis, n):
    total = jnp.sum(jnp.exp(logits - top[:, None]), axis=1)
    b = 1
    while b < n:
        perm = [(c, c ^ b) for c in range(n)]
        other_top = lax.ppermute(top, axis, perm)
        other_total = lax.ppermute(total, axis, perm)
        new_top = jnp.maximum(top, other_top)
        total = total * jnp.exp(top - new_top) + other_total * jnp.exp(other_top - new_top)
        top = new_top
        b *= 2
    return top, total


def two_stage_reduce_scatter(parts, axis, n_hi, n_lo):
    me = lax.axis_index(axis)
    h = me // n_lo
    lo = me % n_lo
    rows = parts.shape[2]
    half = (rows // 2) // 8 * 8
    fwd = parts[:, :, :half, :]
    bwd = parts[:, :, half:, :]
    perm_f = [(a * n_lo + l, a * n_lo + (l + 1) % n_lo) for a in range(n_hi) for l in range(n_lo)]
    perm_b = [(a * n_lo + l, a * n_lo + (l - 1) % n_lo) for a in range(n_hi) for l in range(n_lo)]
    recv_f = recv_b = None
    for s in range(n_lo - 1):
        send_f = lax.dynamic_index_in_dim(fwd, (lo - 1 - s) % n_lo, 1, keepdims=False)
        send_b = lax.dynamic_index_in_dim(bwd, (lo + 1 + s) % n_lo, 1, keepdims=False)
        if recv_f is not None:
            send_f = send_f + recv_f
            send_b = send_b + recv_b
        recv_f = lax.ppermute(send_f, axis, perm_f)
        recv_b = lax.ppermute(send_b, axis, perm_b)
    sum_f = lax.dynamic_index_in_dim(fwd, lo, 1, keepdims=False) + recv_f
    sum_b = lax.dynamic_index_in_dim(bwd, lo, 1, keepdims=False) + recv_b
    perm_h = [(a * n_lo + l, (n_hi - 1 - a) * n_lo + l) for a in range(n_hi) for l in range(n_lo)]
    out_f = lax.dynamic_index_in_dim(sum_f, h, 0, keepdims=False) + lax.ppermute(
        lax.dynamic_index_in_dim(sum_f, n_hi - 1 - h, 0, keepdims=False), axis, perm_h
    )
    out_b = lax.dynamic_index_in_dim(sum_b, h, 0, keepdims=False) + lax.ppermute(
        lax.dynamic_index_in_dim(sum_b, n_hi - 1 - h, 0, keepdims=False), axis, perm_h
    )
    return jnp.concatenate([out_f, out_b], axis=0)


def shards(hidden_input_state, norm_gain, head_weight, target_ids):
    tokens, local_cols = hidden_input_state.shape
    width, vocab_rows = head_weight.shape
    n_tensor = width // local_cols
    n_outer = lax.psum(1, "outer")
    blocks = shift_gather(hidden_input_state.T, "tensor", n_tensor)
    values_t = blocks.reshape(width, tokens).astype(jnp.float32)
    scaled = lax.rsqrt(jnp.mean(values_t * values_t, axis=0) + epsilon)
    scaled_rows = scaled[:, None]
    normalized_t = values_t * scaled[None, :]
    normed_t = (normalized_t * norm_gain[:, None]).astype(jnp.bfloat16)
    logits = lax.dot_general(
        normed_t, head_weight, (((0,), (0,)), ((), ())), preferred_element_type=jnp.float32
    )
    row_top, row_total = butterfly_softmax_stats(
        jnp.max(logits, axis=1), logits, "tensor", n_tensor
    )
    log_total = row_top + jnp.log(row_total)
    offset = lax.axis_index("tensor") * vocab_rows
    column_ids = offset + lax.broadcasted_iota(jnp.int32, (1, vocab_rows), 1)
    onehot = (column_ids == target_ids[:, None]).astype(jnp.float32)
    dlogits = (jnp.exp(logits - log_total[:, None]) - onehot).astype(jnp.bfloat16)

    head_partial = lax.dot_general(
        normed_t, dlogits, (((1,), (0,)), ((), ())), preferred_element_type=jnp.float32
    )
    grad_head = lax.psum_scatter(head_partial, ("outer", "core"), scatter_dimension=0, tiled=True)

    partial = lax.dot_general(
        head_weight, dlogits, (((1,), (1,)), ((), ())), preferred_element_type=jnp.float32
    )
    inner_part = jnp.sum(partial * (norm_gain[:, None] * normalized_t), axis=0)
    gain_part = jnp.sum(partial * normalized_t, axis=1)

    n_lo = 4 if n_tensor % 4 == 0 else n_tensor
    n_hi = n_tensor // n_lo
    gain_rows = -(-local_cols // tokens)
    gain_chunks = jnp.pad(
        gain_part.reshape(n_tensor, local_cols), ((0, 0), (0, gain_rows * tokens - local_cols))
    ).reshape(n_tensor, gain_rows, tokens)
    extra = jnp.concatenate(
        [
            jnp.broadcast_to(inner_part[None, None, :], (n_tensor, 1, tokens)),
            gain_chunks,
            jnp.zeros((n_tensor, 7 - gain_rows, tokens), jnp.float32),
        ],
        axis=1,
    )
    chunks = jnp.concatenate([partial.reshape(n_tensor, local_cols, tokens), extra], axis=1)
    summed = two_stage_reduce_scatter(
        chunks.reshape(n_hi, n_lo, local_cols + 8, tokens), "tensor", n_hi, n_lo
    )
    grad_cols = summed[:local_cols]
    row_inner_sum = summed[local_cols] / width
    gain_local = summed[local_cols + 1 : local_cols + 1 + gain_rows].reshape(-1)[:local_cols]

    normed_gradient = grad_cols.T
    start_col = lax.axis_index("tensor") * local_cols
    normalized_slice = hidden_input_state.astype(jnp.float32) * scaled_rows
    gain_slice = lax.dynamic_slice_in_dim(norm_gain, start_col, local_cols)
    weighted_rows = normed_gradient * gain_slice[None, :]
    hidden_state_gradient = scaled_rows * (
        weighted_rows - normalized_slice * row_inner_sum[:, None]
    )
    norm_gain_gradient = butterfly_sum(butterfly_sum(gain_local, "outer", n_outer), "core", 2)
    return (hidden_state_gradient, grad_head, norm_gain_gradient)


def solution(mesh):
    n_dp, n_tensor = mesh.devices.shape
    split = Mesh(mesh.devices.reshape(n_dp // 2, 2, n_tensor), ("outer", "core", "tensor"))
    dp = ("outer", "core")
    return jax.shard_map(
        shards,
        mesh=split,
        in_specs=(P(dp, "tensor"), P(), P(None, "tensor"), P(dp)),
        out_specs=(P(dp, "tensor"), P(dp, "tensor"), P("tensor")),
        check_vma=False,
    )
```

```python
import jax
import jax.numpy as jnp
from jax import lax
from jax.sharding import Mesh, PartitionSpec as P

epsilon = 1e-06


def shift_gather(x, axis, n):
    me = lax.axis_index(axis)
    got = [x]
    for k in range(1, n):
        got.append(lax.ppermute(x, axis, [(c, (c + k) % n) for c in range(n)]))
    rev = jnp.stack(got[::-1])
    doubled = jnp.concatenate([rev, rev], axis=0)
    return lax.dynamic_slice_in_dim(doubled, (n - 1) - me, n, axis=0)


def butterfly_sum(x, axis, n):
    b = 1
    while b < n:
        x = x + lax.ppermute(x, axis, [(c, c ^ b) for c in range(n)])
        b *= 2
    return x


def butterfly_softmax_stats(top, logits, axis, n):
    total = jnp.sum(jnp.exp(logits - top[:, None]), axis=1)
    b = 1
    while b < n:
        perm = [(c, c ^ b) for c in range(n)]
        other_top = lax.ppermute(top, axis, perm)
        other_total = lax.ppermute(total, axis, perm)
        new_top = jnp.maximum(top, other_top)
        total = total * jnp.exp(top - new_top) + other_total * jnp.exp(other_top - new_top)
        top = new_top
        b *= 2
    return top, total


def two_stage_reduce_scatter(parts, axis, n_hi, n_lo):
    me = lax.axis_index(axis)
    h = me // n_lo
    lo = me % n_lo
    rows = parts.shape[2]
    half = (rows // 2) // 8 * 8
    fwd = parts[:, :, :half, :]
    bwd = parts[:, :, half:, :]
    perm_f = [(a * n_lo + l, a * n_lo + (l + 1) % n_lo) for a in range(n_hi) for l in range(n_lo)]
    perm_b = [(a * n_lo + l, a * n_lo + (l - 1) % n_lo) for a in range(n_hi) for l in range(n_lo)]
    recv_f = recv_b = None
    for s in range(n_lo - 1):
        send_f = lax.dynamic_index_in_dim(fwd, (lo - 1 - s) % n_lo, 1, keepdims=False)
        send_b = lax.dynamic_index_in_dim(bwd, (lo + 1 + s) % n_lo, 1, keepdims=False)
        if recv_f is not None:
            send_f = send_f + recv_f
            send_b = send_b + recv_b
        recv_f = lax.ppermute(send_f, axis, perm_f)
        recv_b = lax.ppermute(send_b, axis, perm_b)
    sum_f = lax.dynamic_index_in_dim(fwd, lo, 1, keepdims=False) + recv_f
    sum_b = lax.dynamic_index_in_dim(bwd, lo, 1, keepdims=False) + recv_b
    perm_h = [(a * n_lo + l, (n_hi - 1 - a) * n_lo + l) for a in range(n_hi) for l in range(n_lo)]
    out_f = lax.dynamic_index_in_dim(sum_f, h, 0, keepdims=False) + lax.ppermute(
        lax.dynamic_index_in_dim(sum_f, n_hi - 1 - h, 0, keepdims=False), axis, perm_h
    )
    out_b = lax.dynamic_index_in_dim(sum_b, h, 0, keepdims=False) + lax.ppermute(
        lax.dynamic_index_in_dim(sum_b, n_hi - 1 - h, 0, keepdims=False), axis, perm_h
    )
    return jnp.concatenate([out_f, out_b], axis=0)


def shards(hidden_input_state, norm_gain, head_weight, target_ids):
    tokens, local_cols = hidden_input_state.shape
    width, vocab_rows = head_weight.shape
    n_tensor = width // local_cols
    n_outer = lax.psum(1, "outer")
    blocks = shift_gather(hidden_input_state.T, "tensor", n_tensor)
    values_t = blocks.reshape(width, tokens).astype(jnp.float32)
    scaled = lax.rsqrt(jnp.mean(values_t * values_t, axis=0) + epsilon)
    scaled_rows = scaled[:, None]
    normalized_t = values_t * scaled[None, :]
    normed_t = (normalized_t * norm_gain[:, None]).astype(jnp.bfloat16)
    logits = lax.dot_general(
        normed_t, head_weight, (((0,), (0,)), ((), ())), preferred_element_type=jnp.float32
    )
    row_top, row_total = butterfly_softmax_stats(
        jnp.max(logits, axis=1), logits, "tensor", n_tensor
    )
    log_total = row_top + jnp.log(row_total)
    offset = lax.axis_index("tensor") * vocab_rows
    column_ids = offset + lax.broadcasted_iota(jnp.int32, (1, vocab_rows), 1)
    onehot = (column_ids == target_ids[:, None]).astype(jnp.float32)
    dlogits = (jnp.exp(logits - log_total[:, None]) - onehot).astype(jnp.bfloat16)

    head_partial = lax.dot_general(
        normed_t, dlogits, (((1,), (0,)), ((), ())), preferred_element_type=jnp.float32
    )
    grad_head = lax.psum_scatter(head_partial, ("outer", "core"), scatter_dimension=0, tiled=True)

    partial = lax.dot_general(
        head_weight.reshape(n_tensor, local_cols, vocab_rows),
        jnp.broadcast_to(dlogits[None], (n_tensor, tokens, vocab_rows)),
        (((2,), (2,)), ((0,), (0,))),
        preferred_element_type=jnp.float32,
    ).reshape(width, tokens)
    inner_part = jnp.sum(partial * (norm_gain[:, None] * normalized_t), axis=0)
    gain_part = jnp.sum(partial * normalized_t, axis=1)

    n_lo = 4 if n_tensor % 4 == 0 else n_tensor
    n_hi = n_tensor // n_lo
    gain_rows = -(-local_cols // tokens)
    gain_chunks = jnp.pad(
        gain_part.reshape(n_tensor, local_cols), ((0, 0), (0, gain_rows * tokens - local_cols))
    ).reshape(n_tensor, gain_rows, tokens)
    extra = jnp.concatenate(
        [
            jnp.broadcast_to(inner_part[None, None, :], (n_tensor, 1, tokens)),
            gain_chunks,
            jnp.zeros((n_tensor, 7 - gain_rows, tokens), jnp.float32),
        ],
        axis=1,
    )
    chunks = jnp.concatenate([partial.reshape(n_tensor, local_cols, tokens), extra], axis=1)
    summed = two_stage_reduce_scatter(
        chunks.reshape(n_hi, n_lo, local_cols + 8, tokens), "tensor", n_hi, n_lo
    )
    grad_cols = summed[:local_cols]
    row_inner_sum = summed[local_cols] / width
    gain_local = summed[local_cols + 1 : local_cols + 1 + gain_rows].reshape(-1)[:local_cols]

    normed_gradient = grad_cols.T
    start_col = lax.axis_index("tensor") * local_cols
    normalized_slice = hidden_input_state.astype(jnp.float32) * scaled_rows
    gain_slice = lax.dynamic_slice_in_dim(norm_gain, start_col, local_cols)
    weighted_rows = normed_gradient * gain_slice[None, :]
    hidden_state_gradient = scaled_rows * (
        weighted_rows - normalized_slice * row_inner_sum[:, None]
    )
    norm_gain_gradient = butterfly_sum(butterfly_sum(gain_local, "outer", n_outer), "core", 2)
    return (hidden_state_gradient, grad_head, norm_gain_gradient)


def solution(mesh):
    n_dp, n_tensor = mesh.devices.shape
    split = Mesh(mesh.devices.reshape(n_dp // 2, 2, n_tensor), ("outer", "core", "tensor"))
    dp = ("outer", "core")
    return jax.shard_map(
        shards,
        mesh=split,
        in_specs=(P(dp, "tensor"), P(), P(None, "tensor"), P(dp)),
        out_specs=(P(dp, "tensor"), P(dp, "tensor"), P("tensor")),
        check_vma=False,
    )
```

```python
import jax
import jax.numpy as jnp
from jax import lax
from jax.sharding import Mesh, PartitionSpec as P

epsilon = 1e-06


def shift_gather(x, axis, n):
    me = lax.axis_index(axis)
    got = [x]
    for k in range(1, n):
        got.append(lax.ppermute(x, axis, [(c, (c + k) % n) for c in range(n)]))
    rev = jnp.stack(got[::-1])
    doubled = jnp.concatenate([rev, rev], axis=0)
    return lax.dynamic_slice_in_dim(doubled, (n - 1) - me, n, axis=0)


def butterfly_sum(x, axis, n):
    b = 1
    while b < n:
        x = x + lax.ppermute(x, axis, [(c, c ^ b) for c in range(n)])
        b *= 2
    return x


def butterfly_softmax_stats(top, logits, axis, n):
    total = jnp.sum(jnp.exp(logits - top[:, None]), axis=1)
    b = 1
    while b < n:
        perm = [(c, c ^ b) for c in range(n)]
        other_top = lax.ppermute(top, axis, perm)
        other_total = lax.ppermute(total, axis, perm)
        new_top = jnp.maximum(top, other_top)
        total = total * jnp.exp(top - new_top) + other_total * jnp.exp(other_top - new_top)
        top = new_top
        b *= 2
    return top, total


def two_stage_reduce_scatter(parts, axis, n_hi, n_lo):
    me = lax.axis_index(axis)
    h = me // n_lo
    lo = me % n_lo
    rows = parts.shape[2]
    half = (rows // 2) // 8 * 8
    fwd = parts[:, :, :half, :]
    bwd = parts[:, :, half:, :]
    perm_f = [(a * n_lo + l, a * n_lo + (l + 1) % n_lo) for a in range(n_hi) for l in range(n_lo)]
    perm_b = [(a * n_lo + l, a * n_lo + (l - 1) % n_lo) for a in range(n_hi) for l in range(n_lo)]
    recv_f = recv_b = None
    for s in range(n_lo - 1):
        send_f = lax.dynamic_index_in_dim(fwd, (lo - 1 - s) % n_lo, 1, keepdims=False)
        send_b = lax.dynamic_index_in_dim(bwd, (lo + 1 + s) % n_lo, 1, keepdims=False)
        if recv_f is not None:
            send_f = send_f + recv_f
            send_b = send_b + recv_b
        recv_f = lax.ppermute(send_f, axis, perm_f)
        recv_b = lax.ppermute(send_b, axis, perm_b)
    sum_f = lax.dynamic_index_in_dim(fwd, lo, 1, keepdims=False) + recv_f
    sum_b = lax.dynamic_index_in_dim(bwd, lo, 1, keepdims=False) + recv_b
    perm_h = [(a * n_lo + l, (n_hi - 1 - a) * n_lo + l) for a in range(n_hi) for l in range(n_lo)]
    out_f = lax.dynamic_index_in_dim(sum_f, h, 0, keepdims=False) + lax.ppermute(
        lax.dynamic_index_in_dim(sum_f, n_hi - 1 - h, 0, keepdims=False), axis, perm_h
    )
    out_b = lax.dynamic_index_in_dim(sum_b, h, 0, keepdims=False) + lax.ppermute(
        lax.dynamic_index_in_dim(sum_b, n_hi - 1 - h, 0, keepdims=False), axis, perm_h
    )
    return jnp.concatenate([out_f, out_b], axis=0)


def shards(hidden_input_state, norm_gain, head_weight, target_ids):
    tokens, local_cols = hidden_input_state.shape
    width, vocab_rows = head_weight.shape
    n_tensor = width // local_cols
    n_outer = lax.psum(1, "outer")
    offset = lax.axis_index("tensor") * vocab_rows
    column_ids = offset + lax.broadcasted_iota(jnp.int32, (1, vocab_rows), 1)

    def front(hidden_t, targets):
        blocks = shift_gather(hidden_t, "tensor", n_tensor)
        values_t = blocks.reshape(width, hidden_t.shape[1]).astype(jnp.float32)
        scaled = lax.rsqrt(jnp.mean(values_t * values_t, axis=0) + epsilon)
        normalized_t = values_t * scaled[None, :]
        normed_t = (normalized_t * norm_gain[:, None]).astype(jnp.bfloat16)
        logits = lax.dot_general(
            normed_t, head_weight, (((0,), (0,)), ((), ())), preferred_element_type=jnp.float32
        )
        local_top = jnp.max(logits, axis=1)
        local_total = jnp.sum(jnp.exp(logits - local_top[:, None]), axis=1)
        stats = shift_gather(jnp.stack([local_top, local_total]), "tensor", n_tensor)
        row_top = jnp.max(stats[:, 0, :], axis=0)
        row_total = jnp.sum(stats[:, 1, :] * jnp.exp(stats[:, 0, :] - row_top[None, :]), axis=0)
        log_total = row_top + jnp.log(row_total)
        onehot = (column_ids == targets[:, None]).astype(jnp.float32)
        dlogits = (jnp.exp(logits - log_total[:, None]) - onehot).astype(jnp.bfloat16)
        head_part = lax.dot_general(
            normed_t, dlogits, (((1,), (0,)), ((), ())), preferred_element_type=jnp.float32
        )
        return scaled, normalized_t, dlogits, head_part

    first = 256 if tokens > 256 and tokens % 128 == 0 else tokens
    hidden_t = hidden_input_state.T
    parts = [front(hidden_t[:, :first], target_ids[:first])]
    if first < tokens:
        parts.append(front(hidden_t[:, first:], target_ids[first:]))
    scaled = jnp.concatenate([p[0] for p in parts])
    scaled_rows = scaled[:, None]
    normalized_t = jnp.concatenate([p[1] for p in parts], axis=1)
    dlogits = jnp.concatenate([p[2] for p in parts], axis=0)
    head_partial = parts[0][3]
    for p in parts[1:]:
        head_partial = head_partial + p[3]
    grad_head = lax.psum_scatter(head_partial, ("outer", "core"), scatter_dimension=0, tiled=True)

    partial = lax.dot_general(
        head_weight.reshape(n_tensor, local_cols, vocab_rows),
        jnp.broadcast_to(dlogits[None], (n_tensor, tokens, vocab_rows)),
        (((2,), (2,)), ((0,), (0,))),
        preferred_element_type=jnp.float32,
    ).reshape(width, tokens)
    inner_part = jnp.sum(partial * (norm_gain[:, None] * normalized_t), axis=0)
    gain_part = jnp.sum(partial * normalized_t, axis=1)

    n_lo = 4 if n_tensor % 4 == 0 else n_tensor
    n_hi = n_tensor // n_lo
    gain_rows = -(-local_cols // tokens)
    gain_chunks = jnp.pad(
        gain_part.reshape(n_tensor, local_cols), ((0, 0), (0, gain_rows * tokens - local_cols))
    ).reshape(n_tensor, gain_rows, tokens)
    extra = jnp.concatenate(
        [
            jnp.broadcast_to(inner_part[None, None, :], (n_tensor, 1, tokens)),
            gain_chunks,
            jnp.zeros((n_tensor, 7 - gain_rows, tokens), jnp.float32),
        ],
        axis=1,
    )
    chunks = jnp.concatenate([partial.reshape(n_tensor, local_cols, tokens), extra], axis=1)
    summed = two_stage_reduce_scatter(
        chunks.reshape(n_hi, n_lo, local_cols + 8, tokens), "tensor", n_hi, n_lo
    )
    grad_cols = summed[:local_cols]
    row_inner_sum = summed[local_cols] / width
    gain_local = summed[local_cols + 1 : local_cols + 1 + gain_rows].reshape(-1)[:local_cols]

    normed_gradient = grad_cols.T
    start_col = lax.axis_index("tensor") * local_cols
    normalized_slice = hidden_input_state.astype(jnp.float32) * scaled_rows
    gain_slice = lax.dynamic_slice_in_dim(norm_gain, start_col, local_cols)
    weighted_rows = normed_gradient * gain_slice[None, :]
    hidden_state_gradient = scaled_rows * (
        weighted_rows - normalized_slice * row_inner_sum[:, None]
    )
    norm_gain_gradient = butterfly_sum(butterfly_sum(gain_local, "outer", n_outer), "core", 2)
    return (hidden_state_gradient, grad_head, norm_gain_gradient)


def solution(mesh):
    n_dp, n_tensor = mesh.devices.shape
    split = Mesh(mesh.devices.reshape(n_dp // 2, 2, n_tensor), ("outer", "core", "tensor"))
    dp = ("outer", "core")
    return jax.shard_map(
        shards,
        mesh=split,
        in_specs=(P(dp, "tensor"), P(), P(None, "tensor"), P(dp)),
        out_specs=(P(dp, "tensor"), P(dp, "tensor"), P("tensor")),
        check_vma=False,
    )
```

```python
import jax
import jax.numpy as jnp
from jax import lax
from jax.sharding import Mesh, PartitionSpec as P

epsilon = 1e-06


def shift_gather(x, axis, n):
    me = lax.axis_index(axis)
    got = [x]
    for k in range(1, n):
        got.append(lax.ppermute(x, axis, [(c, (c + k) % n) for c in range(n)]))
    rev = jnp.stack(got[::-1])
    doubled = jnp.concatenate([rev, rev], axis=0)
    return lax.dynamic_slice_in_dim(doubled, (n - 1) - me, n, axis=0)


def butterfly_sum(x, axis, n):
    b = 1
    while b < n:
        x = x + lax.ppermute(x, axis, [(c, c ^ b) for c in range(n)])
        b *= 2
    return x


def butterfly_softmax_stats(top, logits, axis, n):
    total = jnp.sum(jnp.exp(logits - top[:, None]), axis=1)
    b = 1
    while b < n:
        other = lax.ppermute(jnp.stack([top, total]), axis, [(c, c ^ b) for c in range(n)])
        other_top, other_total = other[0], other[1]
        new_top = jnp.maximum(top, other_top)
        total = total * jnp.exp(top - new_top) + other_total * jnp.exp(other_top - new_top)
        top = new_top
        b *= 2
    return top, total


def two_stage_reduce_scatter(parts, axis, n_hi, n_lo):
    me = lax.axis_index(axis)
    h = me // n_lo
    lo = me % n_lo
    rows = parts.shape[2]
    half = (rows // 2) // 8 * 8
    fwd = parts[:, :, :half, :]
    bwd = parts[:, :, half:, :]
    perm_f = [(a * n_lo + l, a * n_lo + (l + 1) % n_lo) for a in range(n_hi) for l in range(n_lo)]
    perm_b = [(a * n_lo + l, a * n_lo + (l - 1) % n_lo) for a in range(n_hi) for l in range(n_lo)]
    recv_f = recv_b = None
    for s in range(n_lo - 1):
        send_f = lax.dynamic_index_in_dim(fwd, (lo - 1 - s) % n_lo, 1, keepdims=False)
        send_b = lax.dynamic_index_in_dim(bwd, (lo + 1 + s) % n_lo, 1, keepdims=False)
        if recv_f is not None:
            send_f = send_f + recv_f
            send_b = send_b + recv_b
        recv_f = lax.ppermute(send_f, axis, perm_f)
        recv_b = lax.ppermute(send_b, axis, perm_b)
    sum_f = lax.dynamic_index_in_dim(fwd, lo, 1, keepdims=False) + recv_f
    sum_b = lax.dynamic_index_in_dim(bwd, lo, 1, keepdims=False) + recv_b
    both = jnp.concatenate([sum_f, sum_b], axis=1)
    if n_hi == 1:
        return both[0]
    perm_h = [(a * n_lo + l, (n_hi - 1 - a) * n_lo + l) for a in range(n_hi) for l in range(n_lo)]
    return lax.dynamic_index_in_dim(both, h, 0, keepdims=False) + lax.ppermute(
        lax.dynamic_index_in_dim(both, n_hi - 1 - h, 0, keepdims=False), axis, perm_h
    )


def shards(hidden_input_state, norm_gain, head_weight, target_ids):
    tokens, local_cols = hidden_input_state.shape
    width, vocab_rows = head_weight.shape
    n_tensor = width // local_cols
    n_outer = lax.psum(1, "outer")
    blocks = shift_gather(hidden_input_state.T, "tensor", n_tensor)
    values_t = blocks.reshape(width, tokens).astype(jnp.float32)
    scaled = lax.rsqrt(jnp.mean(values_t * values_t, axis=0) + epsilon)
    scaled_rows = scaled[:, None]
    normalized_t = values_t * scaled[None, :]
    normed_t = (normalized_t * norm_gain[:, None]).astype(jnp.bfloat16)
    logits = lax.dot_general(
        normed_t, head_weight, (((0,), (0,)), ((), ())), preferred_element_type=jnp.float32
    )
    row_top, row_total = butterfly_softmax_stats(
        jnp.max(logits, axis=1), logits, "tensor", n_tensor
    )
    log_total = row_top + jnp.log(row_total)
    offset = lax.axis_index("tensor") * vocab_rows
    column_ids = offset + lax.broadcasted_iota(jnp.int32, (1, vocab_rows), 1)
    onehot = (column_ids == target_ids[:, None]).astype(jnp.float32)
    dlogits = (jnp.exp(logits - log_total[:, None]) - onehot).astype(jnp.bfloat16)

    head_partial = lax.dot_general(
        normed_t, dlogits, (((1,), (0,)), ((), ())), preferred_element_type=jnp.float32
    )
    grad_head = lax.psum_scatter(head_partial, ("outer", "core"), scatter_dimension=0, tiled=True)

    partial = lax.dot_general(
        head_weight.reshape(n_tensor, local_cols, vocab_rows),
        jnp.broadcast_to(dlogits[None], (n_tensor, tokens, vocab_rows)),
        (((2,), (2,)), ((0,), (0,))),
        preferred_element_type=jnp.float32,
    ).reshape(width, tokens)
    inner_part = jnp.sum(partial * (norm_gain[:, None] * normalized_t), axis=0)
    gain_part = jnp.sum(partial * normalized_t, axis=1)

    n_lo = 4 if n_tensor % 4 == 0 else n_tensor
    n_hi = n_tensor // n_lo
    gain_rows = -(-local_cols // tokens)
    gain_chunks = jnp.pad(
        gain_part.reshape(n_tensor, local_cols), ((0, 0), (0, gain_rows * tokens - local_cols))
    ).reshape(n_tensor, gain_rows, tokens)
    extra = jnp.concatenate(
        [
            jnp.broadcast_to(inner_part[None, None, :], (n_tensor, 1, tokens)),
            gain_chunks,
            jnp.zeros((n_tensor, 7 - gain_rows, tokens), jnp.float32),
        ],
        axis=1,
    )
    chunks = jnp.concatenate([partial.reshape(n_tensor, local_cols, tokens), extra], axis=1)
    summed = two_stage_reduce_scatter(
        chunks.reshape(n_hi, n_lo, local_cols + 8, tokens), "tensor", n_hi, n_lo
    )
    grad_cols = summed[:local_cols]
    row_inner_sum = summed[local_cols] / width
    gain_local = summed[local_cols + 1 : local_cols + 1 + gain_rows].reshape(-1)[:local_cols]

    normed_gradient = grad_cols.T
    start_col = lax.axis_index("tensor") * local_cols
    normalized_slice = hidden_input_state.astype(jnp.float32) * scaled_rows
    gain_slice = lax.dynamic_slice_in_dim(norm_gain, start_col, local_cols)
    weighted_rows = normed_gradient * gain_slice[None, :]
    hidden_state_gradient = scaled_rows * (
        weighted_rows - normalized_slice * row_inner_sum[:, None]
    )
    norm_gain_gradient = butterfly_sum(butterfly_sum(gain_local, "outer", n_outer), "core", 2)
    return (hidden_state_gradient, grad_head, norm_gain_gradient)


def solution(mesh):
    n_dp, n_tensor = mesh.devices.shape
    split = Mesh(mesh.devices.reshape(n_dp // 2, 2, n_tensor), ("outer", "core", "tensor"))
    dp = ("outer", "core")
    return jax.shard_map(
        shards,
        mesh=split,
        in_specs=(P(dp, "tensor"), P(), P(None, "tensor"), P(dp)),
        out_specs=(P(dp, "tensor"), P(dp, "tensor"), P("tensor")),
        check_vma=False,
    )
```

```python
import jax
import jax.numpy as jnp
from jax import lax
from jax.sharding import Mesh, PartitionSpec as P

epsilon = 1e-06


def shift_gather(x, axis, n):
    me = lax.axis_index(axis)
    got = [x]
    for k in range(1, n):
        got.append(lax.ppermute(x, axis, [(c, (c + k) % n) for c in range(n)]))
    rev = jnp.stack(got[::-1])
    doubled = jnp.concatenate([rev, rev], axis=0)
    return lax.dynamic_slice_in_dim(doubled, (n - 1) - me, n, axis=0)


def butterfly_sum(x, axis, n):
    b = 1
    while b < n:
        x = x + lax.ppermute(x, axis, [(c, c ^ b) for c in range(n)])
        b *= 2
    return x


def butterfly_softmax_stats(top, logits, axis, n):
    total = jnp.sum(jnp.exp(logits - top[:, None]), axis=1)
    b = 1
    while b < n:
        other = lax.ppermute(jnp.stack([top, total]), axis, [(c, c ^ b) for c in range(n)])
        other_top, other_total = other[0], other[1]
        new_top = jnp.maximum(top, other_top)
        total = total * jnp.exp(top - new_top) + other_total * jnp.exp(other_top - new_top)
        top = new_top
        b *= 2
    return top, total


def two_stage_reduce_scatter(parts, axis, n_hi, n_lo):
    me = lax.axis_index(axis)
    h = me // n_lo
    lo = me % n_lo
    rows = parts.shape[2]
    half = (rows // 2) // 8 * 8
    fwd = parts[:, :, :half, :]
    bwd = parts[:, :, half:, :]
    perm_f = [(a * n_lo + l, a * n_lo + (l + 1) % n_lo) for a in range(n_hi) for l in range(n_lo)]
    perm_b = [(a * n_lo + l, a * n_lo + (l - 1) % n_lo) for a in range(n_hi) for l in range(n_lo)]
    recv_f = recv_b = None
    for s in range(n_lo - 1):
        send_f = lax.dynamic_index_in_dim(fwd, (lo - 1 - s) % n_lo, 1, keepdims=False)
        send_b = lax.dynamic_index_in_dim(bwd, (lo + 1 + s) % n_lo, 1, keepdims=False)
        if recv_f is not None:
            send_f = send_f + recv_f
            send_b = send_b + recv_b
        recv_f = lax.ppermute(send_f, axis, perm_f)
        recv_b = lax.ppermute(send_b, axis, perm_b)
    sum_f = lax.dynamic_index_in_dim(fwd, lo, 1, keepdims=False) + recv_f
    sum_b = lax.dynamic_index_in_dim(bwd, lo, 1, keepdims=False) + recv_b
    perm_h = [(a * n_lo + l, (n_hi - 1 - a) * n_lo + l) for a in range(n_hi) for l in range(n_lo)]
    out = []
    for part in (sum_f, sum_b):
        cut = (part.shape[1] // 2) // 8 * 8
        for piece in (part[:, :cut], part[:, cut:]):
            mine = lax.dynamic_index_in_dim(piece, h, 0, keepdims=False)
            if n_hi > 1:
                other = lax.dynamic_index_in_dim(piece, n_hi - 1 - h, 0, keepdims=False)
                mine = mine + lax.ppermute(other, axis, perm_h)
            out.append(mine)
    return jnp.concatenate(out, axis=0)


def shards(hidden_input_state, norm_gain, head_weight, target_ids):
    tokens, local_cols = hidden_input_state.shape
    width, vocab_rows = head_weight.shape
    n_tensor = width // local_cols
    n_outer = lax.psum(1, "outer")
    blocks = shift_gather(hidden_input_state.T, "tensor", n_tensor)
    values_t = blocks.reshape(width, tokens).astype(jnp.float32)
    scaled = lax.rsqrt(jnp.mean(values_t * values_t, axis=0) + epsilon)
    scaled_rows = scaled[:, None]
    normalized_t = values_t * scaled[None, :]
    normed_t = (normalized_t * norm_gain[:, None]).astype(jnp.bfloat16)
    logits = lax.dot_general(
        normed_t, head_weight, (((0,), (0,)), ((), ())), preferred_element_type=jnp.float32
    )
    row_top, row_total = butterfly_softmax_stats(
        jnp.max(logits, axis=1), logits, "tensor", n_tensor
    )
    log_total = row_top + jnp.log(row_total)
    offset = lax.axis_index("tensor") * vocab_rows
    column_ids = offset + lax.broadcasted_iota(jnp.int32, (1, vocab_rows), 1)
    onehot = (column_ids == target_ids[:, None]).astype(jnp.float32)
    dlogits = (jnp.exp(logits - log_total[:, None]) - onehot).astype(jnp.bfloat16)

    head_partial = lax.dot_general(
        normed_t, dlogits, (((1,), (0,)), ((), ())), preferred_element_type=jnp.float32
    )
    grad_head = lax.psum_scatter(head_partial, ("outer", "core"), scatter_dimension=0, tiled=True)

    partial = lax.dot_general(
        head_weight.reshape(n_tensor, local_cols, vocab_rows),
        jnp.broadcast_to(dlogits[None], (n_tensor, tokens, vocab_rows)),
        (((2,), (2,)), ((0,), (0,))),
        preferred_element_type=jnp.float32,
    ).reshape(width, tokens)
    inner_part = jnp.sum(partial * (norm_gain[:, None] * normalized_t), axis=0)
    gain_part = jnp.sum(partial * normalized_t, axis=1)

    n_lo = 4 if n_tensor % 4 == 0 else n_tensor
    n_hi = n_tensor // n_lo
    gain_rows = -(-local_cols // tokens)
    gain_chunks = jnp.pad(
        gain_part.reshape(n_tensor, local_cols), ((0, 0), (0, gain_rows * tokens - local_cols))
    ).reshape(n_tensor, gain_rows, tokens)
    extra = jnp.concatenate(
        [
            jnp.broadcast_to(inner_part[None, None, :], (n_tensor, 1, tokens)),
            gain_chunks,
            jnp.zeros((n_tensor, 7 - gain_rows, tokens), jnp.float32),
        ],
        axis=1,
    )
    chunks = jnp.concatenate([partial.reshape(n_tensor, local_cols, tokens), extra], axis=1)
    summed = two_stage_reduce_scatter(
        chunks.reshape(n_hi, n_lo, local_cols + 8, tokens), "tensor", n_hi, n_lo
    )
    grad_cols = summed[:local_cols]
    row_inner_sum = summed[local_cols] / width
    gain_local = summed[local_cols + 1 : local_cols + 1 + gain_rows].reshape(-1)[:local_cols]

    normed_gradient = grad_cols.T
    start_col = lax.axis_index("tensor") * local_cols
    normalized_slice = hidden_input_state.astype(jnp.float32) * scaled_rows
    gain_slice = lax.dynamic_slice_in_dim(norm_gain, start_col, local_cols)
    weighted_rows = normed_gradient * gain_slice[None, :]
    hidden_state_gradient = scaled_rows * (
        weighted_rows - normalized_slice * row_inner_sum[:, None]
    )
    norm_gain_gradient = butterfly_sum(butterfly_sum(gain_local, "outer", n_outer), "core", 2)
    return (hidden_state_gradient, grad_head, norm_gain_gradient)


def solution(mesh):
    n_dp, n_tensor = mesh.devices.shape
    split = Mesh(mesh.devices.reshape(n_dp // 2, 2, n_tensor), ("outer", "core", "tensor"))
    dp = ("outer", "core")
    return jax.shard_map(
        shards,
        mesh=split,
        in_specs=(P(dp, "tensor"), P(), P(None, "tensor"), P(dp)),
        out_specs=(P(dp, "tensor"), P(dp, "tensor"), P("tensor")),
        check_vma=False,
    )
```

```python
import jax
import jax.numpy as jnp
from jax import lax
from jax.sharding import Mesh, PartitionSpec as P

epsilon = 1e-06


def shift_gather(x, axis, n):
    me = lax.axis_index(axis)
    got = [x]
    for k in range(1, n):
        got.append(lax.ppermute(x, axis, [(c, (c + k) % n) for c in range(n)]))
    rev = jnp.stack(got[::-1])
    doubled = jnp.concatenate([rev, rev], axis=0)
    return lax.dynamic_slice_in_dim(doubled, (n - 1) - me, n, axis=0)


def butterfly_sum(x, axis, n):
    b = 1
    while b < n:
        x = x + lax.ppermute(x, axis, [(c, c ^ b) for c in range(n)])
        b *= 2
    return x


def butterfly_softmax_stats(top, logits, axis, n):
    total = jnp.sum(jnp.exp(logits - top[:, None]), axis=1)
    b = 1
    while b < n:
        other = lax.ppermute(jnp.stack([top, total]), axis, [(c, c ^ b) for c in range(n)])
        other_top, other_total = other[0], other[1]
        new_top = jnp.maximum(top, other_top)
        total = total * jnp.exp(top - new_top) + other_total * jnp.exp(other_top - new_top)
        top = new_top
        b *= 2
    return top, total


def two_stage_reduce_scatter(parts, axis, n_hi, n_lo):
    me = lax.axis_index(axis)
    h = me // n_lo
    lo = me % n_lo
    rows = parts.shape[2]
    half = (rows // 2) // 8 * 8
    fwd = parts[:, :, :half, :]
    bwd = parts[:, :, half:, :]
    perm_f = [(a * n_lo + l, a * n_lo + (l + 1) % n_lo) for a in range(n_hi) for l in range(n_lo)]
    perm_b = [(a * n_lo + l, a * n_lo + (l - 1) % n_lo) for a in range(n_hi) for l in range(n_lo)]
    recv_f = recv_b = None
    for s in range(n_lo - 1):
        send_f = lax.dynamic_index_in_dim(fwd, (lo - 1 - s) % n_lo, 1, keepdims=False)
        send_b = lax.dynamic_index_in_dim(bwd, (lo + 1 + s) % n_lo, 1, keepdims=False)
        if recv_f is not None:
            send_f = send_f + recv_f
            send_b = send_b + recv_b
        recv_f = lax.ppermute(send_f, axis, perm_f)
        recv_b = lax.ppermute(send_b, axis, perm_b)
    sum_f = lax.dynamic_index_in_dim(fwd, lo, 1, keepdims=False) + recv_f
    sum_b = lax.dynamic_index_in_dim(bwd, lo, 1, keepdims=False) + recv_b
    perm_h = [(a * n_lo + l, (n_hi - 1 - a) * n_lo + l) for a in range(n_hi) for l in range(n_lo)]
    out = []
    for part in (sum_f, sum_b):
        cut = (part.shape[1] // 2) // 8 * 8
        for piece in (part[:, :cut], part[:, cut:]):
            mine = lax.dynamic_index_in_dim(piece, h, 0, keepdims=False)
            if n_hi > 1:
                other = lax.dynamic_index_in_dim(piece, n_hi - 1 - h, 0, keepdims=False)
                mine = mine + lax.ppermute(other, axis, perm_h)
            out.append(mine)
    return jnp.concatenate(out, axis=0)


def shards(hidden_input_state, norm_gain, head_weight, target_ids):
    tokens, local_cols = hidden_input_state.shape
    width, vocab_rows = head_weight.shape
    n_tensor = width // local_cols
    n_outer = lax.psum(1, "outer")
    blocks = shift_gather(hidden_input_state.T, "tensor", n_tensor)
    values_t = blocks.reshape(width, tokens).astype(jnp.float32)
    scaled = lax.rsqrt(jnp.mean(values_t * values_t, axis=0) + epsilon)
    scaled_rows = scaled[:, None]
    normalized_t = values_t * scaled[None, :]
    normed_t = (normalized_t * norm_gain[:, None]).astype(jnp.bfloat16)
    logits = lax.dot_general(
        normed_t, head_weight, (((0,), (0,)), ((), ())), preferred_element_type=jnp.float32
    )
    row_top, row_total = butterfly_softmax_stats(
        jnp.max(logits, axis=1), logits, "tensor", n_tensor
    )
    log_total = row_top + jnp.log(row_total)
    offset = lax.axis_index("tensor") * vocab_rows
    column_ids = offset + lax.broadcasted_iota(jnp.int32, (1, vocab_rows), 1)
    onehot = (column_ids == target_ids[:, None]).astype(jnp.float32)
    dlogits = (jnp.exp(logits - log_total[:, None]) - onehot).astype(jnp.bfloat16)

    split_at = vocab_rows // 2 if vocab_rows % 256 == 0 else vocab_rows
    halves = []
    for lo, hi in ((0, split_at), (split_at, vocab_rows)):
        if hi > lo:
            head_partial = lax.dot_general(
                normed_t, dlogits[:, lo:hi], (((1,), (0,)), ((), ())),
                preferred_element_type=jnp.float32,
            )
            halves.append(
                lax.psum_scatter(head_partial, ("outer", "core"), scatter_dimension=0, tiled=True)
            )
    grad_head = jnp.concatenate(halves, axis=1)

    partial = lax.dot_general(
        head_weight.reshape(n_tensor, local_cols, vocab_rows),
        jnp.broadcast_to(dlogits[None], (n_tensor, tokens, vocab_rows)),
        (((2,), (2,)), ((0,), (0,))),
        preferred_element_type=jnp.float32,
    ).reshape(width, tokens)
    inner_part = jnp.sum(partial * (norm_gain[:, None] * normalized_t), axis=0)
    gain_part = jnp.sum(partial * normalized_t, axis=1)

    n_lo = 4 if n_tensor % 4 == 0 else n_tensor
    n_hi = n_tensor // n_lo
    gain_rows = -(-local_cols // tokens)
    gain_chunks = jnp.pad(
        gain_part.reshape(n_tensor, local_cols), ((0, 0), (0, gain_rows * tokens - local_cols))
    ).reshape(n_tensor, gain_rows, tokens)
    extra = jnp.concatenate(
        [
            jnp.broadcast_to(inner_part[None, None, :], (n_tensor, 1, tokens)),
            gain_chunks,
            jnp.zeros((n_tensor, 7 - gain_rows, tokens), jnp.float32),
        ],
        axis=1,
    )
    chunks = jnp.concatenate([partial.reshape(n_tensor, local_cols, tokens), extra], axis=1)
    summed = two_stage_reduce_scatter(
        chunks.reshape(n_hi, n_lo, local_cols + 8, tokens), "tensor", n_hi, n_lo
    )
    grad_cols = summed[:local_cols]
    row_inner_sum = summed[local_cols] / width
    gain_local = summed[local_cols + 1 : local_cols + 1 + gain_rows].reshape(-1)[:local_cols]

    normed_gradient = grad_cols.T
    start_col = lax.axis_index("tensor") * local_cols
    normalized_slice = hidden_input_state.astype(jnp.float32) * scaled_rows
    gain_slice = lax.dynamic_slice_in_dim(norm_gain, start_col, local_cols)
    weighted_rows = normed_gradient * gain_slice[None, :]
    hidden_state_gradient = scaled_rows * (
        weighted_rows - normalized_slice * row_inner_sum[:, None]
    )
    norm_gain_gradient = butterfly_sum(butterfly_sum(gain_local, "outer", n_outer), "core", 2)
    return (hidden_state_gradient, grad_head, norm_gain_gradient)


def solution(mesh):
    n_dp, n_tensor = mesh.devices.shape
    split = Mesh(mesh.devices.reshape(n_dp // 2, 2, n_tensor), ("outer", "core", "tensor"))
    dp = ("outer", "core")
    return jax.shard_map(
        shards,
        mesh=split,
        in_specs=(P(dp, "tensor"), P(), P(None, "tensor"), P(dp)),
        out_specs=(P(dp, "tensor"), P(dp, "tensor"), P("tensor")),
        check_vma=False,
    )
```

```python
import jax
import jax.numpy as jnp
from jax import lax
from jax.sharding import Mesh, PartitionSpec as P

epsilon = 1e-06


def shift_gather(x, axis, n):
    me = lax.axis_index(axis)
    got = [x]
    for k in range(1, n):
        got.append(lax.ppermute(x, axis, [(c, (c + k) % n) for c in range(n)]))
    rev = jnp.stack(got[::-1])
    doubled = jnp.concatenate([rev, rev], axis=0)
    return lax.dynamic_slice_in_dim(doubled, (n - 1) - me, n, axis=0)


def butterfly_sum(x, axis, n):
    b = 1
    while b < n:
        x = x + lax.ppermute(x, axis, [(c, c ^ b) for c in range(n)])
        b *= 2
    return x


def group_softmax_stats(top, logits, axis, n_hi, n_lo):
    total = jnp.sum(jnp.exp(logits - top[:, None]), axis=1)
    me = lax.axis_index(axis)
    lo = me % n_lo
    packed = jnp.stack([top, total])
    got = [packed]
    for k in range(1, n_lo):
        perm = [(a * n_lo + l, a * n_lo + (l + k) % n_lo) for a in range(n_hi) for l in range(n_lo)]
        got.append(lax.ppermute(packed, axis, perm))
    rev = jnp.stack(got[::-1])
    ordered = lax.dynamic_slice_in_dim(jnp.concatenate([rev, rev], axis=0), (n_lo - 1) - lo, n_lo, axis=0)
    top = jnp.max(ordered[:, 0, :], axis=0)
    total = jnp.sum(ordered[:, 1, :] * jnp.exp(ordered[:, 0, :] - top[None, :]), axis=0)
    b = n_lo
    while b < n_hi * n_lo:
        other = lax.ppermute(
            jnp.stack([top, total]), axis, [(c, c ^ b) for c in range(n_hi * n_lo)]
        )
        new_top = jnp.maximum(top, other[0])
        total = total * jnp.exp(top - new_top) + other[1] * jnp.exp(other[0] - new_top)
        top = new_top
        b *= 2
    return top, total


def two_stage_reduce_scatter(parts, axis, n_hi, n_lo):
    me = lax.axis_index(axis)
    h = me // n_lo
    lo = me % n_lo
    rows = parts.shape[2]
    half = (rows // 2) // 8 * 8
    fwd = parts[:, :, :half, :]
    bwd = parts[:, :, half:, :]
    perm_f = [(a * n_lo + l, a * n_lo + (l + 1) % n_lo) for a in range(n_hi) for l in range(n_lo)]
    perm_b = [(a * n_lo + l, a * n_lo + (l - 1) % n_lo) for a in range(n_hi) for l in range(n_lo)]
    recv_f = recv_b = None
    for s in range(n_lo - 1):
        send_f = lax.dynamic_index_in_dim(fwd, (lo - 1 - s) % n_lo, 1, keepdims=False)
        send_b = lax.dynamic_index_in_dim(bwd, (lo + 1 + s) % n_lo, 1, keepdims=False)
        if recv_f is not None:
            send_f = send_f + recv_f
            send_b = send_b + recv_b
        recv_f = lax.ppermute(send_f, axis, perm_f)
        recv_b = lax.ppermute(send_b, axis, perm_b)
    sum_f = lax.dynamic_index_in_dim(fwd, lo, 1, keepdims=False) + recv_f
    sum_b = lax.dynamic_index_in_dim(bwd, lo, 1, keepdims=False) + recv_b
    perm_h = [(a * n_lo + l, (n_hi - 1 - a) * n_lo + l) for a in range(n_hi) for l in range(n_lo)]
    out = []
    for part in (sum_f, sum_b):
        cut = (part.shape[1] // 2) // 8 * 8
        for piece in (part[:, :cut], part[:, cut:]):
            mine = lax.dynamic_index_in_dim(piece, h, 0, keepdims=False)
            if n_hi > 1:
                other = lax.dynamic_index_in_dim(piece, n_hi - 1 - h, 0, keepdims=False)
                mine = mine + lax.ppermute(other, axis, perm_h)
            out.append(mine)
    return jnp.concatenate(out, axis=0)


def shards(hidden_input_state, norm_gain, head_weight, target_ids):
    tokens, local_cols = hidden_input_state.shape
    width, vocab_rows = head_weight.shape
    n_tensor = width // local_cols
    n_outer = lax.psum(1, "outer")
    blocks = shift_gather(hidden_input_state.T, "tensor", n_tensor)
    values_t = blocks.reshape(width, tokens).astype(jnp.float32)
    scaled = lax.rsqrt(jnp.mean(values_t * values_t, axis=0) + epsilon)
    scaled_rows = scaled[:, None]
    normalized_t = values_t * scaled[None, :]
    normed_t = (normalized_t * norm_gain[:, None]).astype(jnp.bfloat16)
    logits = lax.dot_general(
        normed_t, head_weight, (((0,), (0,)), ((), ())), preferred_element_type=jnp.float32
    )
    n_lo = 4 if n_tensor % 4 == 0 else n_tensor
    n_hi = n_tensor // n_lo
    row_top, row_total = group_softmax_stats(
        jnp.max(logits, axis=1), logits, "tensor", n_hi, n_lo
    )
    log_total = row_top + jnp.log(row_total)
    offset = lax.axis_index("tensor") * vocab_rows
    column_ids = offset + lax.broadcasted_iota(jnp.int32, (1, vocab_rows), 1)
    onehot = (column_ids == target_ids[:, None]).astype(jnp.float32)
    dlogits = (jnp.exp(logits - log_total[:, None]) - onehot).astype(jnp.bfloat16)

    head_partial = lax.dot_general(
        normed_t, dlogits, (((1,), (0,)), ((), ())), preferred_element_type=jnp.float32
    )
    grad_head = lax.psum_scatter(head_partial, ("outer", "core"), scatter_dimension=0, tiled=True)

    partial = lax.dot_general(
        head_weight.reshape(n_tensor, local_cols, vocab_rows),
        jnp.broadcast_to(dlogits[None], (n_tensor, tokens, vocab_rows)),
        (((2,), (2,)), ((0,), (0,))),
        preferred_element_type=jnp.float32,
    ).reshape(width, tokens)
    inner_part = jnp.sum(partial * (norm_gain[:, None] * normalized_t), axis=0)
    gain_part = jnp.sum(partial * normalized_t, axis=1)

    gain_rows = -(-local_cols // tokens)
    gain_chunks = jnp.pad(
        gain_part.reshape(n_tensor, local_cols), ((0, 0), (0, gain_rows * tokens - local_cols))
    ).reshape(n_tensor, gain_rows, tokens)
    extra = jnp.concatenate(
        [
            jnp.broadcast_to(inner_part[None, None, :], (n_tensor, 1, tokens)),
            gain_chunks,
            jnp.zeros((n_tensor, 7 - gain_rows, tokens), jnp.float32),
        ],
        axis=1,
    )
    chunks = jnp.concatenate([partial.reshape(n_tensor, local_cols, tokens), extra], axis=1)
    summed = two_stage_reduce_scatter(
        chunks.reshape(n_hi, n_lo, local_cols + 8, tokens), "tensor", n_hi, n_lo
    )
    grad_cols = summed[:local_cols]
    row_inner_sum = summed[local_cols] / width
    gain_local = summed[local_cols + 1 : local_cols + 1 + gain_rows].reshape(-1)[:local_cols]

    normed_gradient = grad_cols.T
    start_col = lax.axis_index("tensor") * local_cols
    normalized_slice = hidden_input_state.astype(jnp.float32) * scaled_rows
    gain_slice = lax.dynamic_slice_in_dim(norm_gain, start_col, local_cols)
    weighted_rows = normed_gradient * gain_slice[None, :]
    hidden_state_gradient = scaled_rows * (
        weighted_rows - normalized_slice * row_inner_sum[:, None]
    )
    norm_gain_gradient = butterfly_sum(butterfly_sum(gain_local, "outer", n_outer), "core", 2)
    return (hidden_state_gradient, grad_head, norm_gain_gradient)


def solution(mesh):
    n_dp, n_tensor = mesh.devices.shape
    split = Mesh(mesh.devices.reshape(n_dp // 2, 2, n_tensor), ("outer", "core", "tensor"))
    dp = ("outer", "core")
    return jax.shard_map(
        shards,
        mesh=split,
        in_specs=(P(dp, "tensor"), P(), P(None, "tensor"), P(dp)),
        out_specs=(P(dp, "tensor"), P(dp, "tensor"), P("tensor")),
        check_vma=False,
    )
```

```python
import jax
import jax.numpy as jnp
from jax import lax
from jax.sharding import Mesh, PartitionSpec as P

epsilon = 1e-06


def shift_gather(x, axis, n):
    me = lax.axis_index(axis)
    got = [x]
    for k in range(1, n):
        got.append(lax.ppermute(x, axis, [(c, (c + k) % n) for c in range(n)]))
    rev = jnp.stack(got[::-1])
    doubled = jnp.concatenate([rev, rev], axis=0)
    return lax.dynamic_slice_in_dim(doubled, (n - 1) - me, n, axis=0)


def grid_gather(x, axis, n_hi, n_lo):
    me = lax.axis_index(axis)
    h = me // n_lo
    lo = me % n_lo
    got = {}
    offsets = [(a, b) for a in range(n_hi) for b in range(n_lo) if (a, b) != (0, 0)]
    offsets.sort(key=lambda o: -o[0])
    for a, b in offsets:
        perm = [
            (p * n_lo + q, ((p + a) % n_hi) * n_lo + (q + b) % n_lo)
            for p in range(n_hi)
            for q in range(n_lo)
        ]
        got[(a, b)] = lax.ppermute(x, axis, perm)
    got[(0, 0)] = x
    rev = jnp.stack(
        [jnp.stack([got[(n_hi - 1 - a, n_lo - 1 - b)] for b in range(n_lo)]) for a in range(n_hi)]
    )
    doubled = jnp.concatenate([rev, rev], axis=0)
    doubled = jnp.concatenate([doubled, doubled], axis=1)
    ordered = lax.dynamic_slice_in_dim(doubled, (n_hi - 1) - h, n_hi, axis=0)
    ordered = lax.dynamic_slice_in_dim(ordered, (n_lo - 1) - lo, n_lo, axis=1)
    return ordered.reshape((n_hi * n_lo,) + x.shape)


def butterfly_sum(x, axis, n):
    b = 1
    while b < n:
        x = x + lax.ppermute(x, axis, [(c, c ^ b) for c in range(n)])
        b *= 2
    return x


def butterfly_softmax_stats(top, logits, axis, n):
    total = jnp.sum(jnp.exp(logits - top[:, None]), axis=1)
    b = 1
    while b < n:
        other = lax.ppermute(jnp.stack([top, total]), axis, [(c, c ^ b) for c in range(n)])
        other_top, other_total = other[0], other[1]
        new_top = jnp.maximum(top, other_top)
        total = total * jnp.exp(top - new_top) + other_total * jnp.exp(other_top - new_top)
        top = new_top
        b *= 2
    return top, total


def two_stage_reduce_scatter(parts, axis, n_hi, n_lo):
    me = lax.axis_index(axis)
    h = me // n_lo
    lo = me % n_lo
    rows = parts.shape[2]
    half = (rows // 2) // 8 * 8
    fwd = parts[:, :, :half, :]
    bwd = parts[:, :, half:, :]
    perm_f = [(a * n_lo + l, a * n_lo + (l + 1) % n_lo) for a in range(n_hi) for l in range(n_lo)]
    perm_b = [(a * n_lo + l, a * n_lo + (l - 1) % n_lo) for a in range(n_hi) for l in range(n_lo)]
    recv_f = recv_b = None
    for s in range(n_lo - 1):
        send_f = lax.dynamic_index_in_dim(fwd, (lo - 1 - s) % n_lo, 1, keepdims=False)
        send_b = lax.dynamic_index_in_dim(bwd, (lo + 1 + s) % n_lo, 1, keepdims=False)
        if recv_f is not None:
            send_f = send_f + recv_f
            send_b = send_b + recv_b
        recv_f = lax.ppermute(send_f, axis, perm_f)
        recv_b = lax.ppermute(send_b, axis, perm_b)
    sum_f = lax.dynamic_index_in_dim(fwd, lo, 1, keepdims=False) + recv_f
    sum_b = lax.dynamic_index_in_dim(bwd, lo, 1, keepdims=False) + recv_b
    perm_h = [(a * n_lo + l, (n_hi - 1 - a) * n_lo + l) for a in range(n_hi) for l in range(n_lo)]
    out = []
    for part in (sum_f, sum_b):
        cut = (part.shape[1] // 2) // 8 * 8
        for piece in (part[:, :cut], part[:, cut:]):
            mine = lax.dynamic_index_in_dim(piece, h, 0, keepdims=False)
            if n_hi > 1:
                other = lax.dynamic_index_in_dim(piece, n_hi - 1 - h, 0, keepdims=False)
                mine = mine + lax.ppermute(other, axis, perm_h)
            out.append(mine)
    return jnp.concatenate(out, axis=0)


def shards(hidden_input_state, norm_gain, head_weight, target_ids):
    tokens, local_cols = hidden_input_state.shape
    width, vocab_rows = head_weight.shape
    n_tensor = width // local_cols
    n_outer = lax.psum(1, "outer")
    n_lo = 4 if n_tensor % 4 == 0 else n_tensor
    n_hi = n_tensor // n_lo
    blocks = grid_gather(hidden_input_state.T, "tensor", n_hi, n_lo)
    values_t = blocks.reshape(width, tokens).astype(jnp.float32)
    scaled = lax.rsqrt(jnp.mean(values_t * values_t, axis=0) + epsilon)
    scaled_rows = scaled[:, None]
    normalized_t = values_t * scaled[None, :]
    normed_t = (normalized_t * norm_gain[:, None]).astype(jnp.bfloat16)
    logits = lax.dot_general(
        normed_t, head_weight, (((0,), (0,)), ((), ())), preferred_element_type=jnp.float32
    )
    row_top, row_total = butterfly_softmax_stats(
        jnp.max(logits, axis=1), logits, "tensor", n_tensor
    )
    log_total = row_top + jnp.log(row_total)
    offset = lax.axis_index("tensor") * vocab_rows
    column_ids = offset + lax.broadcasted_iota(jnp.int32, (1, vocab_rows), 1)
    onehot = (column_ids == target_ids[:, None]).astype(jnp.float32)
    dlogits = (jnp.exp(logits - log_total[:, None]) - onehot).astype(jnp.bfloat16)

    head_partial = lax.dot_general(
        normed_t, dlogits, (((1,), (0,)), ((), ())), preferred_element_type=jnp.float32
    )
    grad_head = lax.psum_scatter(head_partial, ("outer", "core"), scatter_dimension=0, tiled=True)

    partial = lax.dot_general(
        head_weight.reshape(n_tensor, local_cols, vocab_rows),
        jnp.broadcast_to(dlogits[None], (n_tensor, tokens, vocab_rows)),
        (((2,), (2,)), ((0,), (0,))),
        preferred_element_type=jnp.float32,
    ).reshape(width, tokens)
    inner_part = jnp.sum(partial * (norm_gain[:, None] * normalized_t), axis=0)
    gain_part = jnp.sum(partial * normalized_t, axis=1)

    gain_rows = -(-local_cols // tokens)
    gain_chunks = jnp.pad(
        gain_part.reshape(n_tensor, local_cols), ((0, 0), (0, gain_rows * tokens - local_cols))
    ).reshape(n_tensor, gain_rows, tokens)
    extra = jnp.concatenate(
        [
            jnp.broadcast_to(inner_part[None, None, :], (n_tensor, 1, tokens)),
            gain_chunks,
            jnp.zeros((n_tensor, 7 - gain_rows, tokens), jnp.float32),
        ],
        axis=1,
    )
    chunks = jnp.concatenate([partial.reshape(n_tensor, local_cols, tokens), extra], axis=1)
    summed = two_stage_reduce_scatter(
        chunks.reshape(n_hi, n_lo, local_cols + 8, tokens), "tensor", n_hi, n_lo
    )
    grad_cols = summed[:local_cols]
    row_inner_sum = summed[local_cols] / width
    gain_local = summed[local_cols + 1 : local_cols + 1 + gain_rows].reshape(-1)[:local_cols]

    normed_gradient = grad_cols.T
    start_col = lax.axis_index("tensor") * local_cols
    normalized_slice = hidden_input_state.astype(jnp.float32) * scaled_rows
    gain_slice = lax.dynamic_slice_in_dim(norm_gain, start_col, local_cols)
    weighted_rows = normed_gradient * gain_slice[None, :]
    hidden_state_gradient = scaled_rows * (
        weighted_rows - normalized_slice * row_inner_sum[:, None]
    )
    norm_gain_gradient = butterfly_sum(butterfly_sum(gain_local, "outer", n_outer), "core", 2)
    return (hidden_state_gradient, grad_head, norm_gain_gradient)


def solution(mesh):
    n_dp, n_tensor = mesh.devices.shape
    split = Mesh(mesh.devices.reshape(n_dp // 2, 2, n_tensor), ("outer", "core", "tensor"))
    dp = ("outer", "core")
    return jax.shard_map(
        shards,
        mesh=split,
        in_specs=(P(dp, "tensor"), P(), P(None, "tensor"), P(dp)),
        out_specs=(P(dp, "tensor"), P(dp, "tensor"), P("tensor")),
        check_vma=False,
    )
```

```python
import jax
import jax.numpy as jnp
from jax import lax
from jax.sharding import Mesh, PartitionSpec as P

epsilon = 1e-06


def shift_gather(x, axis, n):
    me = lax.axis_index(axis)
    got = [x]
    for k in range(1, n):
        got.append(lax.ppermute(x, axis, [(c, (c + k) % n) for c in range(n)]))
    rev = jnp.stack(got[::-1])
    doubled = jnp.concatenate([rev, rev], axis=0)
    return lax.dynamic_slice_in_dim(doubled, (n - 1) - me, n, axis=0)


def grid_gather(x, axis, n_hi, n_lo):
    me = lax.axis_index(axis)
    h = me // n_lo
    lo = me % n_lo
    got = {}
    offsets = [(a, b) for a in range(n_hi) for b in range(n_lo) if (a, b) != (0, 0)]
    offsets.sort(key=lambda o: -o[0])
    for a, b in offsets:
        perm = [
            (p * n_lo + q, ((p + a) % n_hi) * n_lo + (q + b) % n_lo)
            for p in range(n_hi)
            for q in range(n_lo)
        ]
        got[(a, b)] = lax.ppermute(x, axis, perm)
    got[(0, 0)] = x
    rev = jnp.stack(
        [jnp.stack([got[(n_hi - 1 - a, n_lo - 1 - b)] for b in range(n_lo)]) for a in range(n_hi)]
    )
    doubled = jnp.concatenate([rev, rev], axis=0)
    doubled = jnp.concatenate([doubled, doubled], axis=1)
    ordered = lax.dynamic_slice_in_dim(doubled, (n_hi - 1) - h, n_hi, axis=0)
    ordered = lax.dynamic_slice_in_dim(ordered, (n_lo - 1) - lo, n_lo, axis=1)
    return ordered.reshape((n_hi * n_lo,) + x.shape)


def butterfly_sum(x, axis, n):
    b = 1
    while b < n:
        x = x + lax.ppermute(x, axis, [(c, c ^ b) for c in range(n)])
        b *= 2
    return x


def butterfly_softmax_stats(top, logits, axis, n):
    total = jnp.sum(jnp.exp(logits - top[:, None]), axis=1)
    b = 1
    while b < n:
        other = lax.ppermute(jnp.stack([top, total]), axis, [(c, c ^ b) for c in range(n)])
        other_top, other_total = other[0], other[1]
        new_top = jnp.maximum(top, other_top)
        total = total * jnp.exp(top - new_top) + other_total * jnp.exp(other_top - new_top)
        top = new_top
        b *= 2
    return top, total


def two_stage_reduce_scatter(parts, axis, n_hi, n_lo):
    me = lax.axis_index(axis)
    h = me // n_lo
    lo = me % n_lo
    rows = parts.shape[2]
    half = (rows // 2) // 8 * 8
    fwd = parts[:, :, :half, :]
    bwd = parts[:, :, half:, :]
    perm_f = [(a * n_lo + l, a * n_lo + (l + 1) % n_lo) for a in range(n_hi) for l in range(n_lo)]
    perm_b = [(a * n_lo + l, a * n_lo + (l - 1) % n_lo) for a in range(n_hi) for l in range(n_lo)]
    recv_f = recv_b = None
    for s in range(n_lo - 1):
        send_f = lax.dynamic_index_in_dim(fwd, (lo - 1 - s) % n_lo, 1, keepdims=False)
        send_b = lax.dynamic_index_in_dim(bwd, (lo + 1 + s) % n_lo, 1, keepdims=False)
        if recv_f is not None:
            send_f = send_f + recv_f
            send_b = send_b + recv_b
        recv_f = lax.ppermute(send_f, axis, perm_f)
        recv_b = lax.ppermute(send_b, axis, perm_b)
    sum_f = lax.dynamic_index_in_dim(fwd, lo, 1, keepdims=False) + recv_f
    sum_b = lax.dynamic_index_in_dim(bwd, lo, 1, keepdims=False) + recv_b
    perm_h = [(a * n_lo + l, (n_hi - 1 - a) * n_lo + l) for a in range(n_hi) for l in range(n_lo)]
    out = []
    for part in (sum_f, sum_b):
        cut = (part.shape[1] // 2) // 8 * 8
        for piece in (part[:, :cut], part[:, cut:]):
            mine = lax.dynamic_index_in_dim(piece, h, 0, keepdims=False)
            if n_hi > 1:
                other = lax.dynamic_index_in_dim(piece, n_hi - 1 - h, 0, keepdims=False)
                mine = mine + lax.ppermute(other, axis, perm_h)
            out.append(mine)
    return jnp.concatenate(out, axis=0)


def shards(hidden_input_state, norm_gain, head_weight, target_ids):
    tokens, local_cols = hidden_input_state.shape
    width, vocab_rows = head_weight.shape
    n_tensor = width // local_cols
    n_outer = lax.psum(1, "outer")
    n_lo = 4 if n_tensor % 4 == 0 else n_tensor
    n_hi = n_tensor // n_lo
    blocks = grid_gather(hidden_input_state.T, "tensor", n_hi, n_lo)
    values_t = blocks.reshape(width, tokens).astype(jnp.float32)
    scaled = lax.rsqrt(jnp.mean(values_t * values_t, axis=0) + epsilon)
    scaled_rows = scaled[:, None]
    normalized_t = values_t * scaled[None, :]
    normed_t = (normalized_t * norm_gain[:, None]).astype(jnp.bfloat16)
    logits = lax.dot_general(
        normed_t, head_weight, (((0,), (0,)), ((), ())), preferred_element_type=jnp.float32
    )
    row_top, row_total = butterfly_softmax_stats(
        jnp.max(logits, axis=1), logits, "tensor", n_tensor
    )
    log_total = row_top + jnp.log(row_total)
    offset = lax.axis_index("tensor") * vocab_rows
    column_ids = offset + lax.broadcasted_iota(jnp.int32, (1, vocab_rows), 1)
    onehot = (column_ids == target_ids[:, None]).astype(jnp.float32)
    dlogits = (jnp.exp(logits - log_total[:, None]) - onehot).astype(jnp.bfloat16)

    core = lax.axis_index("core")
    by_core = normed_t.reshape(n_outer, 2, width // (2 * n_outer), tokens)

    def head_rows(which):
        rows = lax.dynamic_index_in_dim(by_core, which, 1, keepdims=False).reshape(width // 2, tokens)
        return lax.dot_general(
            rows, dlogits, (((1,), (0,)), ((), ())), preferred_element_type=jnp.float32
        )

    sent = lax.ppermute(head_rows(1 - core), "core", [(0, 1), (1, 0)])
    kept = head_rows(core) + sent
    grad_head = lax.psum_scatter(kept, "outer", scatter_dimension=0, tiled=True)

    partial = lax.dot_general(
        head_weight.reshape(n_tensor, local_cols, vocab_rows),
        jnp.broadcast_to(dlogits[None], (n_tensor, tokens, vocab_rows)),
        (((2,), (2,)), ((0,), (0,))),
        preferred_element_type=jnp.float32,
    ).reshape(width, tokens)
    inner_part = jnp.sum(partial * (norm_gain[:, None] * normalized_t), axis=0)
    gain_part = jnp.sum(partial * normalized_t, axis=1)

    gain_rows = -(-local_cols // tokens)
    gain_chunks = jnp.pad(
        gain_part.reshape(n_tensor, local_cols), ((0, 0), (0, gain_rows * tokens - local_cols))
    ).reshape(n_tensor, gain_rows, tokens)
    extra = jnp.concatenate(
        [
            jnp.broadcast_to(inner_part[None, None, :], (n_tensor, 1, tokens)),
            gain_chunks,
            jnp.zeros((n_tensor, 7 - gain_rows, tokens), jnp.float32),
        ],
        axis=1,
    )
    chunks = jnp.concatenate([partial.reshape(n_tensor, local_cols, tokens), extra], axis=1)
    summed = two_stage_reduce_scatter(
        chunks.reshape(n_hi, n_lo, local_cols + 8, tokens), "tensor", n_hi, n_lo
    )
    grad_cols = summed[:local_cols]
    row_inner_sum = summed[local_cols] / width
    gain_local = summed[local_cols + 1 : local_cols + 1 + gain_rows].reshape(-1)[:local_cols]

    normed_gradient = grad_cols.T
    start_col = lax.axis_index("tensor") * local_cols
    normalized_slice = hidden_input_state.astype(jnp.float32) * scaled_rows
    gain_slice = lax.dynamic_slice_in_dim(norm_gain, start_col, local_cols)
    weighted_rows = normed_gradient * gain_slice[None, :]
    hidden_state_gradient = scaled_rows * (
        weighted_rows - normalized_slice * row_inner_sum[:, None]
    )
    norm_gain_gradient = butterfly_sum(butterfly_sum(gain_local, "outer", n_outer), "core", 2)
    return (hidden_state_gradient, grad_head, norm_gain_gradient)


def solution(mesh):
    n_dp, n_tensor = mesh.devices.shape
    split = Mesh(mesh.devices.reshape(n_dp // 2, 2, n_tensor), ("outer", "core", "tensor"))
    dp = ("outer", "core")
    return jax.shard_map(
        shards,
        mesh=split,
        in_specs=(P(dp, "tensor"), P(), P(None, "tensor"), P(dp)),
        out_specs=(P(dp, "tensor"), P(dp, "tensor"), P("tensor")),
        check_vma=False,
    )
```

```python
import jax
import jax.numpy as jnp
from jax import lax
from jax.sharding import Mesh, PartitionSpec as P

epsilon = 1e-06


def shift_gather(x, axis, n):
    me = lax.axis_index(axis)
    got = [x]
    for k in range(1, n):
        got.append(lax.ppermute(x, axis, [(c, (c + k) % n) for c in range(n)]))
    rev = jnp.stack(got[::-1])
    doubled = jnp.concatenate([rev, rev], axis=0)
    return lax.dynamic_slice_in_dim(doubled, (n - 1) - me, n, axis=0)


def grid_gather(x, axis, n_hi, n_lo):
    me = lax.axis_index(axis)
    h = me // n_lo
    lo = me % n_lo
    got = {}
    offsets = [(a, b) for a in range(n_hi) for b in range(n_lo) if (a, b) != (0, 0)]
    offsets.sort(key=lambda o: -o[0])
    for a, b in offsets:
        perm = [
            (p * n_lo + q, ((p + a) % n_hi) * n_lo + (q + b) % n_lo)
            for p in range(n_hi)
            for q in range(n_lo)
        ]
        got[(a, b)] = lax.ppermute(x, axis, perm)
    got[(0, 0)] = x
    rev = jnp.stack(
        [jnp.stack([got[(n_hi - 1 - a, n_lo - 1 - b)] for b in range(n_lo)]) for a in range(n_hi)]
    )
    doubled = jnp.concatenate([rev, rev], axis=0)
    doubled = jnp.concatenate([doubled, doubled], axis=1)
    ordered = lax.dynamic_slice_in_dim(doubled, (n_hi - 1) - h, n_hi, axis=0)
    ordered = lax.dynamic_slice_in_dim(ordered, (n_lo - 1) - lo, n_lo, axis=1)
    return ordered.reshape((n_hi * n_lo,) + x.shape)


def butterfly_sum(x, axis, n):
    b = 1
    while b < n:
        x = x + lax.ppermute(x, axis, [(c, c ^ b) for c in range(n)])
        b *= 2
    return x


def butterfly_softmax_stats(top, logits, axis, n):
    total = jnp.sum(jnp.exp(logits - top[:, None]), axis=1)
    b = 1
    while b < n:
        other = lax.ppermute(jnp.stack([top, total]), axis, [(c, c ^ b) for c in range(n)])
        other_top, other_total = other[0], other[1]
        new_top = jnp.maximum(top, other_top)
        total = total * jnp.exp(top - new_top) + other_total * jnp.exp(other_top - new_top)
        top = new_top
        b *= 2
    return top, total


def two_stage_reduce_scatter(parts, axis, n_hi, n_lo):
    me = lax.axis_index(axis)
    h = me // n_lo
    lo = me % n_lo
    rows = parts.shape[2]
    half = (rows // 2) // 8 * 8
    fwd = parts[:, :, :half, :]
    bwd = parts[:, :, half:, :]
    perm_f = [(a * n_lo + l, a * n_lo + (l + 1) % n_lo) for a in range(n_hi) for l in range(n_lo)]
    perm_b = [(a * n_lo + l, a * n_lo + (l - 1) % n_lo) for a in range(n_hi) for l in range(n_lo)]
    recv_f = recv_b = None
    for s in range(n_lo - 1):
        send_f = lax.dynamic_index_in_dim(fwd, (lo - 1 - s) % n_lo, 1, keepdims=False)
        send_b = lax.dynamic_index_in_dim(bwd, (lo + 1 + s) % n_lo, 1, keepdims=False)
        if recv_f is not None:
            send_f = send_f + recv_f
            send_b = send_b + recv_b
        recv_f = lax.ppermute(send_f, axis, perm_f)
        recv_b = lax.ppermute(send_b, axis, perm_b)
    sum_f = lax.dynamic_index_in_dim(fwd, lo, 1, keepdims=False) + recv_f
    sum_b = lax.dynamic_index_in_dim(bwd, lo, 1, keepdims=False) + recv_b
    perm_h = [(a * n_lo + l, (n_hi - 1 - a) * n_lo + l) for a in range(n_hi) for l in range(n_lo)]
    out = []
    for part in (sum_f, sum_b):
        cut = (part.shape[1] // 2) // 8 * 8
        for piece in (part[:, :cut], part[:, cut:]):
            mine = lax.dynamic_index_in_dim(piece, h, 0, keepdims=False)
            if n_hi > 1:
                other = lax.dynamic_index_in_dim(piece, n_hi - 1 - h, 0, keepdims=False)
                mine = mine + lax.ppermute(other, axis, perm_h)
            out.append(mine)
    return jnp.concatenate(out, axis=0)


def shards(hidden_input_state, norm_gain, head_weight, target_ids):
    tokens, local_cols = hidden_input_state.shape
    width, vocab_rows = head_weight.shape
    n_tensor = width // local_cols
    n_outer = lax.psum(1, "outer")
    n_lo = 4 if n_tensor % 4 == 0 else n_tensor
    n_hi = n_tensor // n_lo
    blocks = grid_gather(hidden_input_state.T, "tensor", n_hi, n_lo)
    values_t = blocks.reshape(width, tokens).astype(jnp.float32)
    scaled = lax.rsqrt(jnp.mean(values_t * values_t, axis=0) + epsilon)
    scaled_rows = scaled[:, None]
    normalized_t = values_t * scaled[None, :]
    normed_t = (normalized_t * norm_gain[:, None]).astype(jnp.bfloat16)
    logits = lax.dot_general(
        normed_t, head_weight, (((0,), (0,)), ((), ())), preferred_element_type=jnp.float32
    )
    row_top, row_total = butterfly_softmax_stats(
        jnp.max(logits, axis=1), logits, "tensor", n_tensor
    )
    log_total = row_top + jnp.log(row_total)
    offset = lax.axis_index("tensor") * vocab_rows
    column_ids = offset + lax.broadcasted_iota(jnp.int32, (1, vocab_rows), 1)
    onehot = (column_ids == target_ids[:, None]).astype(jnp.float32)
    dlogits = (jnp.exp(logits - log_total[:, None]) - onehot).astype(jnp.bfloat16)

    core = lax.axis_index("core")
    by_core = normed_t.reshape(n_outer, 2, width // (2 * n_outer), tokens)

    def head_rows(which, by_core):
        rows = lax.dynamic_index_in_dim(by_core, which, 1, keepdims=False).reshape(width // 2, tokens)
        return lax.dot_general(
            rows, dlogits, (((1,), (0,)), ((), ())), preferred_element_type=jnp.float32
        )

    sent = lax.ppermute(head_rows(1 - core, by_core), "core", [(0, 1), (1, 0)])

    partial = lax.dot_general(
        head_weight.reshape(n_tensor, local_cols, vocab_rows),
        jnp.broadcast_to(dlogits[None], (n_tensor, tokens, vocab_rows)),
        (((2,), (2,)), ((0,), (0,))),
        preferred_element_type=jnp.float32,
    ).reshape(width, tokens)
    inner_part = jnp.sum(partial * (norm_gain[:, None] * normalized_t), axis=0)
    gain_part = jnp.sum(partial * normalized_t, axis=1)
    partial, inner_part, gain_part, by_core = lax.optimization_barrier(
        (partial, inner_part, gain_part, by_core)
    )
    kept = head_rows(core, by_core) + sent
    grad_head = lax.psum_scatter(kept, "outer", scatter_dimension=0, tiled=True)

    gain_rows = -(-local_cols // tokens)
    gain_chunks = jnp.pad(
        gain_part.reshape(n_tensor, local_cols), ((0, 0), (0, gain_rows * tokens - local_cols))
    ).reshape(n_tensor, gain_rows, tokens)
    extra = jnp.concatenate(
        [
            jnp.broadcast_to(inner_part[None, None, :], (n_tensor, 1, tokens)),
            gain_chunks,
            jnp.zeros((n_tensor, 7 - gain_rows, tokens), jnp.float32),
        ],
        axis=1,
    )
    chunks = jnp.concatenate([partial.reshape(n_tensor, local_cols, tokens), extra], axis=1)
    summed = two_stage_reduce_scatter(
        chunks.reshape(n_hi, n_lo, local_cols + 8, tokens), "tensor", n_hi, n_lo
    )
    grad_cols = summed[:local_cols]
    row_inner_sum = summed[local_cols] / width
    gain_local = summed[local_cols + 1 : local_cols + 1 + gain_rows].reshape(-1)[:local_cols]

    normed_gradient = grad_cols.T
    start_col = lax.axis_index("tensor") * local_cols
    normalized_slice = hidden_input_state.astype(jnp.float32) * scaled_rows
    gain_slice = lax.dynamic_slice_in_dim(norm_gain, start_col, local_cols)
    weighted_rows = normed_gradient * gain_slice[None, :]
    hidden_state_gradient = scaled_rows * (
        weighted_rows - normalized_slice * row_inner_sum[:, None]
    )
    norm_gain_gradient = butterfly_sum(butterfly_sum(gain_local, "outer", n_outer), "core", 2)
    return (hidden_state_gradient, grad_head, norm_gain_gradient)


def solution(mesh):
    n_dp, n_tensor = mesh.devices.shape
    split = Mesh(mesh.devices.reshape(n_dp // 2, 2, n_tensor), ("outer", "core", "tensor"))
    dp = ("outer", "core")
    return jax.shard_map(
        shards,
        mesh=split,
        in_specs=(P(dp, "tensor"), P(), P(None, "tensor"), P(dp)),
        out_specs=(P(dp, "tensor"), P(dp, "tensor"), P("tensor")),
        check_vma=False,
    )
```

```python
import jax
import jax.numpy as jnp
from jax import lax
from jax.sharding import Mesh, PartitionSpec as P

epsilon = 1e-06


def shift_gather(x, axis, n):
    me = lax.axis_index(axis)
    got = [x]
    for k in range(1, n):
        got.append(lax.ppermute(x, axis, [(c, (c + k) % n) for c in range(n)]))
    rev = jnp.stack(got[::-1])
    doubled = jnp.concatenate([rev, rev], axis=0)
    return lax.dynamic_slice_in_dim(doubled, (n - 1) - me, n, axis=0)


def grid_gather(x, axis, n_hi, n_lo):
    me = lax.axis_index(axis)
    h = me // n_lo
    lo = me % n_lo
    got = {}
    offsets = [(a, b) for a in range(n_hi) for b in range(n_lo) if (a, b) != (0, 0)]
    offsets.sort(key=lambda o: -o[0])
    for a, b in offsets:
        perm = [
            (p * n_lo + q, ((p + a) % n_hi) * n_lo + (q + b) % n_lo)
            for p in range(n_hi)
            for q in range(n_lo)
        ]
        got[(a, b)] = lax.ppermute(x, axis, perm)
    got[(0, 0)] = x
    rev = jnp.stack(
        [jnp.stack([got[(n_hi - 1 - a, n_lo - 1 - b)] for b in range(n_lo)]) for a in range(n_hi)]
    )
    doubled = jnp.concatenate([rev, rev], axis=0)
    doubled = jnp.concatenate([doubled, doubled], axis=1)
    ordered = lax.dynamic_slice_in_dim(doubled, (n_hi - 1) - h, n_hi, axis=0)
    ordered = lax.dynamic_slice_in_dim(ordered, (n_lo - 1) - lo, n_lo, axis=1)
    return ordered.reshape((n_hi * n_lo,) + x.shape)


def butterfly_sum(x, axis, n):
    b = 1
    while b < n:
        x = x + lax.ppermute(x, axis, [(c, c ^ b) for c in range(n)])
        b *= 2
    return x


def butterfly_softmax_stats(top, logits, axis, n):
    total = jnp.sum(jnp.exp(logits - top[:, None]), axis=1)
    b = 1
    while b < n:
        other = lax.ppermute(jnp.stack([top, total]), axis, [(c, c ^ b) for c in range(n)])
        other_top, other_total = other[0], other[1]
        new_top = jnp.maximum(top, other_top)
        total = total * jnp.exp(top - new_top) + other_total * jnp.exp(other_top - new_top)
        top = new_top
        b *= 2
    return top, total


def two_stage_reduce_scatter(parts, axis, n_hi, n_lo):
    me = lax.axis_index(axis)
    h = me // n_lo
    lo = me % n_lo
    rows = parts.shape[2]
    half = (rows // 2) // 8 * 8
    fwd = parts[:, :, :half, :]
    bwd = parts[:, :, half:, :]
    perm_f = [(a * n_lo + l, a * n_lo + (l + 1) % n_lo) for a in range(n_hi) for l in range(n_lo)]
    perm_b = [(a * n_lo + l, a * n_lo + (l - 1) % n_lo) for a in range(n_hi) for l in range(n_lo)]
    recv_f = recv_b = None
    for s in range(n_lo - 1):
        send_f = lax.dynamic_index_in_dim(fwd, (lo - 1 - s) % n_lo, 1, keepdims=False)
        send_b = lax.dynamic_index_in_dim(bwd, (lo + 1 + s) % n_lo, 1, keepdims=False)
        if recv_f is not None:
            send_f = send_f + recv_f
            send_b = send_b + recv_b
        recv_f = lax.ppermute(send_f, axis, perm_f)
        recv_b = lax.ppermute(send_b, axis, perm_b)
    sum_f = lax.dynamic_index_in_dim(fwd, lo, 1, keepdims=False) + recv_f
    sum_b = lax.dynamic_index_in_dim(bwd, lo, 1, keepdims=False) + recv_b
    perm_h = [(a * n_lo + l, (n_hi - 1 - a) * n_lo + l) for a in range(n_hi) for l in range(n_lo)]
    out = []
    for part in (sum_f, sum_b):
        step = (part.shape[1] // 4) // 8 * 8
        cuts = [0, step, 2 * step, 3 * step, part.shape[1]]
        for piece in [part[:, cuts[i] : cuts[i + 1]] for i in range(4)]:
            mine = lax.dynamic_index_in_dim(piece, h, 0, keepdims=False)
            if n_hi > 1:
                other = lax.dynamic_index_in_dim(piece, n_hi - 1 - h, 0, keepdims=False)
                mine = mine + lax.ppermute(other, axis, perm_h)
            out.append(mine)
    return jnp.concatenate(out, axis=0)


def shards(hidden_input_state, norm_gain, head_weight, target_ids):
    tokens, local_cols = hidden_input_state.shape
    width, vocab_rows = head_weight.shape
    n_tensor = width // local_cols
    n_outer = lax.psum(1, "outer")
    n_lo = 4 if n_tensor % 4 == 0 else n_tensor
    n_hi = n_tensor // n_lo
    blocks = grid_gather(hidden_input_state.T, "tensor", n_hi, n_lo)
    values_t = blocks.reshape(width, tokens).astype(jnp.float32)
    scaled = lax.rsqrt(jnp.mean(values_t * values_t, axis=0) + epsilon)
    scaled_rows = scaled[:, None]
    normalized_t = values_t * scaled[None, :]
    normed_t = (normalized_t * norm_gain[:, None]).astype(jnp.bfloat16)
    logits = lax.dot_general(
        normed_t, head_weight, (((0,), (0,)), ((), ())), preferred_element_type=jnp.float32
    )
    row_top, row_total = butterfly_softmax_stats(
        jnp.max(logits, axis=1), logits, "tensor", n_tensor
    )
    log_total = row_top + jnp.log(row_total)
    offset = lax.axis_index("tensor") * vocab_rows
    column_ids = offset + lax.broadcasted_iota(jnp.int32, (1, vocab_rows), 1)
    onehot = (column_ids == target_ids[:, None]).astype(jnp.float32)
    dlogits = (jnp.exp(logits - log_total[:, None]) - onehot).astype(jnp.bfloat16)

    core = lax.axis_index("core")
    by_core = normed_t.reshape(n_outer, 2, width // (2 * n_outer), tokens)

    def head_rows(which):
        rows = lax.dynamic_index_in_dim(by_core, which, 1, keepdims=False).reshape(width // 2, tokens)
        return lax.dot_general(
            rows, dlogits, (((1,), (0,)), ((), ())), preferred_element_type=jnp.float32
        )

    sent = lax.ppermute(head_rows(1 - core), "core", [(0, 1), (1, 0)])
    kept = head_rows(core) + sent
    grad_head = lax.psum_scatter(kept, "outer", scatter_dimension=0, tiled=True)

    partial = lax.dot_general(
        head_weight.reshape(n_tensor, local_cols, vocab_rows),
        jnp.broadcast_to(dlogits[None], (n_tensor, tokens, vocab_rows)),
        (((2,), (2,)), ((0,), (0,))),
        preferred_element_type=jnp.float32,
    ).reshape(width, tokens)
    inner_part = jnp.sum(partial * (norm_gain[:, None] * normalized_t), axis=0)
    gain_part = jnp.sum(partial * normalized_t, axis=1)

    gain_rows = -(-local_cols // tokens)
    gain_chunks = jnp.pad(
        gain_part.reshape(n_tensor, local_cols), ((0, 0), (0, gain_rows * tokens - local_cols))
    ).reshape(n_tensor, gain_rows, tokens)
    extra = jnp.concatenate(
        [
            jnp.broadcast_to(inner_part[None, None, :], (n_tensor, 1, tokens)),
            gain_chunks,
            jnp.zeros((n_tensor, 7 - gain_rows, tokens), jnp.float32),
        ],
        axis=1,
    )
    chunks = jnp.concatenate([partial.reshape(n_tensor, local_cols, tokens), extra], axis=1)
    summed = two_stage_reduce_scatter(
        chunks.reshape(n_hi, n_lo, local_cols + 8, tokens), "tensor", n_hi, n_lo
    )
    grad_cols = summed[:local_cols]
    row_inner_sum = summed[local_cols] / width
    gain_local = summed[local_cols + 1 : local_cols + 1 + gain_rows].reshape(-1)[:local_cols]

    normed_gradient = grad_cols.T
    start_col = lax.axis_index("tensor") * local_cols
    normalized_slice = hidden_input_state.astype(jnp.float32) * scaled_rows
    gain_slice = lax.dynamic_slice_in_dim(norm_gain, start_col, local_cols)
    weighted_rows = normed_gradient * gain_slice[None, :]
    hidden_state_gradient = scaled_rows * (
        weighted_rows - normalized_slice * row_inner_sum[:, None]
    )
    norm_gain_gradient = butterfly_sum(butterfly_sum(gain_local, "outer", n_outer), "core", 2)
    return (hidden_state_gradient, grad_head, norm_gain_gradient)


def solution(mesh):
    n_dp, n_tensor = mesh.devices.shape
    split = Mesh(mesh.devices.reshape(n_dp // 2, 2, n_tensor), ("outer", "core", "tensor"))
    dp = ("outer", "core")
    return jax.shard_map(
        shards,
        mesh=split,
        in_specs=(P(dp, "tensor"), P(), P(None, "tensor"), P(dp)),
        out_specs=(P(dp, "tensor"), P(dp, "tensor"), P("tensor")),
        check_vma=False,
    )
```

```python
import jax
import jax.numpy as jnp
from jax import lax
from jax.sharding import Mesh, PartitionSpec as P

epsilon = 1e-06


def shift_gather(x, axis, n):
    me = lax.axis_index(axis)
    got = [x]
    for k in range(1, n):
        got.append(lax.ppermute(x, axis, [(c, (c + k) % n) for c in range(n)]))
    rev = jnp.stack(got[::-1])
    doubled = jnp.concatenate([rev, rev], axis=0)
    return lax.dynamic_slice_in_dim(doubled, (n - 1) - me, n, axis=0)


def grid_gather(x, axis, n_hi, n_lo):
    me = lax.axis_index(axis)
    h = me // n_lo
    lo = me % n_lo
    got = {}
    offsets = [(a, b) for a in range(n_hi) for b in range(n_lo) if (a, b) != (0, 0)]
    offsets.sort(key=lambda o: -o[0])
    for a, b in offsets:
        perm = [
            (p * n_lo + q, ((p + a) % n_hi) * n_lo + (q + b) % n_lo)
            for p in range(n_hi)
            for q in range(n_lo)
        ]
        got[(a, b)] = lax.ppermute(x, axis, perm)
    got[(0, 0)] = x
    rev = jnp.stack(
        [jnp.stack([got[(n_hi - 1 - a, n_lo - 1 - b)] for b in range(n_lo)]) for a in range(n_hi)]
    )
    doubled = jnp.concatenate([rev, rev], axis=0)
    doubled = jnp.concatenate([doubled, doubled], axis=1)
    ordered = lax.dynamic_slice_in_dim(doubled, (n_hi - 1) - h, n_hi, axis=0)
    ordered = lax.dynamic_slice_in_dim(ordered, (n_lo - 1) - lo, n_lo, axis=1)
    return ordered.reshape((n_hi * n_lo,) + x.shape)


def butterfly_sum(x, axis, n):
    b = 1
    while b < n:
        x = x + lax.ppermute(x, axis, [(c, c ^ b) for c in range(n)])
        b *= 2
    return x


def group_softmax_stats(top, logits, axis, n_hi, n_lo):
    total = jnp.sum(jnp.exp(logits - top[:, None]), axis=1)
    me = lax.axis_index(axis)
    lo = me % n_lo
    packed = jnp.stack([top, total])
    got = [packed]
    for k in range(1, n_lo):
        perm = [(a * n_lo + l, a * n_lo + (l + k) % n_lo) for a in range(n_hi) for l in range(n_lo)]
        got.append(lax.ppermute(packed, axis, perm))
    rev = jnp.stack(got[::-1])
    doubled = jnp.concatenate([rev, rev], axis=0)
    ordered = lax.dynamic_slice_in_dim(doubled, (n_lo - 1) - lo, n_lo, axis=0)
    top = jnp.max(ordered[:, 0, :], axis=0)
    total = jnp.sum(ordered[:, 1, :] * jnp.exp(ordered[:, 0, :] - top[None, :]), axis=0)
    b = n_lo
    while b < n_hi * n_lo:
        other = lax.ppermute(
            jnp.stack([top, total]), axis, [(c, c ^ b) for c in range(n_hi * n_lo)]
        )
        new_top = jnp.maximum(top, other[0])
        total = total * jnp.exp(top - new_top) + other[1] * jnp.exp(other[0] - new_top)
        top = new_top
        b *= 2
    return top, total


def two_stage_reduce_scatter(parts, axis, n_hi, n_lo):
    me = lax.axis_index(axis)
    h = me // n_lo
    lo = me % n_lo
    rows = parts.shape[2]
    half = (rows // 2) // 8 * 8
    fwd = parts[:, :, :half, :]
    bwd = parts[:, :, half:, :]
    perm_f = [(a * n_lo + l, a * n_lo + (l + 1) % n_lo) for a in range(n_hi) for l in range(n_lo)]
    perm_b = [(a * n_lo + l, a * n_lo + (l - 1) % n_lo) for a in range(n_hi) for l in range(n_lo)]
    recv_f = recv_b = None
    for s in range(n_lo - 1):
        send_f = lax.dynamic_index_in_dim(fwd, (lo - 1 - s) % n_lo, 1, keepdims=False)
        send_b = lax.dynamic_index_in_dim(bwd, (lo + 1 + s) % n_lo, 1, keepdims=False)
        if recv_f is not None:
            send_f = send_f + recv_f
            send_b = send_b + recv_b
        recv_f = lax.ppermute(send_f, axis, perm_f)
        recv_b = lax.ppermute(send_b, axis, perm_b)
    sum_f = lax.dynamic_index_in_dim(fwd, lo, 1, keepdims=False) + recv_f
    sum_b = lax.dynamic_index_in_dim(bwd, lo, 1, keepdims=False) + recv_b
    perm_h = [(a * n_lo + l, (n_hi - 1 - a) * n_lo + l) for a in range(n_hi) for l in range(n_lo)]
    out = []
    for part in (sum_f, sum_b):
        cut = (part.shape[1] // 2) // 8 * 8
        for piece in (part[:, :cut], part[:, cut:]):
            mine = lax.dynamic_index_in_dim(piece, h, 0, keepdims=False)
            if n_hi > 1:
                other = lax.dynamic_index_in_dim(piece, n_hi - 1 - h, 0, keepdims=False)
                mine = mine + lax.ppermute(other, axis, perm_h)
            out.append(mine)
    return jnp.concatenate(out, axis=0)


def shards(hidden_input_state, norm_gain, head_weight, target_ids):
    tokens, local_cols = hidden_input_state.shape
    width, vocab_rows = head_weight.shape
    n_tensor = width // local_cols
    n_outer = lax.psum(1, "outer")
    n_lo = 4 if n_tensor % 4 == 0 else n_tensor
    n_hi = n_tensor // n_lo
    blocks = grid_gather(hidden_input_state.T, "tensor", n_hi, n_lo)
    values_t = blocks.reshape(width, tokens).astype(jnp.float32)
    scaled = lax.rsqrt(jnp.mean(values_t * values_t, axis=0) + epsilon)
    scaled_rows = scaled[:, None]
    normalized_t = values_t * scaled[None, :]
    normed_t = (normalized_t * norm_gain[:, None]).astype(jnp.bfloat16)
    logits = lax.dot_general(
        normed_t, head_weight, (((0,), (0,)), ((), ())), preferred_element_type=jnp.float32
    )
    row_top, row_total = group_softmax_stats(
        jnp.max(logits, axis=1), logits, "tensor", n_hi, n_lo
    )
    log_total = row_top + jnp.log(row_total)
    offset = lax.axis_index("tensor") * vocab_rows
    column_ids = offset + lax.broadcasted_iota(jnp.int32, (1, vocab_rows), 1)
    onehot = (column_ids == target_ids[:, None]).astype(jnp.float32)
    dlogits = (jnp.exp(logits - log_total[:, None]) - onehot).astype(jnp.bfloat16)

    core = lax.axis_index("core")
    by_core = normed_t.reshape(n_outer, 2, width // (2 * n_outer), tokens)

    def head_rows(which):
        rows = lax.dynamic_index_in_dim(by_core, which, 1, keepdims=False).reshape(width // 2, tokens)
        return lax.dot_general(
            rows, dlogits, (((1,), (0,)), ((), ())), preferred_element_type=jnp.float32
        )

    sent = lax.ppermute(head_rows(1 - core), "core", [(0, 1), (1, 0)])
    kept = head_rows(core) + sent
    grad_head = lax.psum_scatter(kept, "outer", scatter_dimension=0, tiled=True)

    partial = lax.dot_general(
        head_weight.reshape(n_tensor, local_cols, vocab_rows),
        jnp.broadcast_to(dlogits[None], (n_tensor, tokens, vocab_rows)),
        (((2,), (2,)), ((0,), (0,))),
        preferred_element_type=jnp.float32,
    ).reshape(width, tokens)
    inner_part = jnp.sum(partial * (norm_gain[:, None] * normalized_t), axis=0)
    gain_part = jnp.sum(partial * normalized_t, axis=1)

    gain_rows = -(-local_cols // tokens)
    gain_chunks = jnp.pad(
        gain_part.reshape(n_tensor, local_cols), ((0, 0), (0, gain_rows * tokens - local_cols))
    ).reshape(n_tensor, gain_rows, tokens)
    extra = jnp.concatenate(
        [
            jnp.broadcast_to(inner_part[None, None, :], (n_tensor, 1, tokens)),
            gain_chunks,
            jnp.zeros((n_tensor, 7 - gain_rows, tokens), jnp.float32),
        ],
        axis=1,
    )
    chunks = jnp.concatenate([partial.reshape(n_tensor, local_cols, tokens), extra], axis=1)
    summed = two_stage_reduce_scatter(
        chunks.reshape(n_hi, n_lo, local_cols + 8, tokens), "tensor", n_hi, n_lo
    )
    grad_cols = summed[:local_cols]
    row_inner_sum = summed[local_cols] / width
    gain_local = summed[local_cols + 1 : local_cols + 1 + gain_rows].reshape(-1)[:local_cols]

    normed_gradient = grad_cols.T
    start_col = lax.axis_index("tensor") * local_cols
    normalized_slice = hidden_input_state.astype(jnp.float32) * scaled_rows
    gain_slice = lax.dynamic_slice_in_dim(norm_gain, start_col, local_cols)
    weighted_rows = normed_gradient * gain_slice[None, :]
    hidden_state_gradient = scaled_rows * (
        weighted_rows - normalized_slice * row_inner_sum[:, None]
    )
    norm_gain_gradient = butterfly_sum(butterfly_sum(gain_local, "outer", n_outer), "core", 2)
    return (hidden_state_gradient, grad_head, norm_gain_gradient)


def solution(mesh):
    n_dp, n_tensor = mesh.devices.shape
    split = Mesh(mesh.devices.reshape(n_dp // 2, 2, n_tensor), ("outer", "core", "tensor"))
    dp = ("outer", "core")
    return jax.shard_map(
        shards,
        mesh=split,
        in_specs=(P(dp, "tensor"), P(), P(None, "tensor"), P(dp)),
        out_specs=(P(dp, "tensor"), P(dp, "tensor"), P("tensor")),
        check_vma=False,
    )
```

```python
import jax
import jax.numpy as jnp
from jax import lax
from jax.sharding import Mesh, PartitionSpec as P

epsilon = 1e-06


def shift_gather(x, axis, n):
    me = lax.axis_index(axis)
    got = [x]
    for k in range(1, n):
        got.append(lax.ppermute(x, axis, [(c, (c + k) % n) for c in range(n)]))
    rev = jnp.stack(got[::-1])
    doubled = jnp.concatenate([rev, rev], axis=0)
    return lax.dynamic_slice_in_dim(doubled, (n - 1) - me, n, axis=0)


def grid_gather(x, axis, n_hi, n_lo):
    me = lax.axis_index(axis)
    h = me // n_lo
    lo = me % n_lo
    got = {}
    offsets = [(a, b) for a in range(n_hi) for b in range(n_lo) if (a, b) != (0, 0)]
    offsets.sort(key=lambda o: -o[0])
    for a, b in offsets:
        perm = [
            (p * n_lo + q, ((p + a) % n_hi) * n_lo + (q + b) % n_lo)
            for p in range(n_hi)
            for q in range(n_lo)
        ]
        got[(a, b)] = lax.ppermute(x, axis, perm)
    got[(0, 0)] = x
    rev = jnp.stack(
        [jnp.stack([got[(n_hi - 1 - a, n_lo - 1 - b)] for b in range(n_lo)]) for a in range(n_hi)]
    )
    doubled = jnp.concatenate([rev, rev], axis=0)
    doubled = jnp.concatenate([doubled, doubled], axis=1)
    ordered = lax.dynamic_slice_in_dim(doubled, (n_hi - 1) - h, n_hi, axis=0)
    ordered = lax.dynamic_slice_in_dim(ordered, (n_lo - 1) - lo, n_lo, axis=1)
    return ordered.reshape((n_hi * n_lo,) + x.shape)


def butterfly_sum(x, axis, n):
    b = 1
    while b < n:
        x = x + lax.ppermute(x, axis, [(c, c ^ b) for c in range(n)])
        b *= 2
    return x


def butterfly_softmax_stats(top, logits, axis, n):
    total = jnp.sum(jnp.exp(logits - top[:, None]), axis=1)
    b = 1
    while b < n:
        other = lax.ppermute(jnp.stack([top, total]), axis, [(c, c ^ b) for c in range(n)])
        other_top, other_total = other[0], other[1]
        new_top = jnp.maximum(top, other_top)
        total = total * jnp.exp(top - new_top) + other_total * jnp.exp(other_top - new_top)
        top = new_top
        b *= 2
    return top, total


def two_stage_reduce_scatter(parts, axis, n_hi, n_lo):
    me = lax.axis_index(axis)
    h = me // n_lo
    lo = me % n_lo
    rows = parts.shape[2]
    half = (rows // 2) // 8 * 8
    fwd = parts[:, :, :half, :]
    bwd = parts[:, :, half:, :]
    perm_f = [(a * n_lo + l, a * n_lo + (l + 1) % n_lo) for a in range(n_hi) for l in range(n_lo)]
    perm_b = [(a * n_lo + l, a * n_lo + (l - 1) % n_lo) for a in range(n_hi) for l in range(n_lo)]
    recv_f = recv_b = None
    for s in range(n_lo - 1):
        send_f = lax.dynamic_index_in_dim(fwd, (lo - 1 - s) % n_lo, 1, keepdims=False)
        send_b = lax.dynamic_index_in_dim(bwd, (lo + 1 + s) % n_lo, 1, keepdims=False)
        if recv_f is not None:
            send_f = send_f + recv_f
            send_b = send_b + recv_b
        recv_f = lax.ppermute(send_f, axis, perm_f)
        recv_b = lax.ppermute(send_b, axis, perm_b)
    sum_f = lax.dynamic_index_in_dim(fwd, lo, 1, keepdims=False) + recv_f
    sum_b = lax.dynamic_index_in_dim(bwd, lo, 1, keepdims=False) + recv_b
    perm_h = [(a * n_lo + l, (n_hi - 1 - a) * n_lo + l) for a in range(n_hi) for l in range(n_lo)]
    out = []
    for part in (sum_f, sum_b):
        for piece in (part,):
            mine = lax.dynamic_index_in_dim(piece, h, 0, keepdims=False)
            if n_hi > 1:
                other = lax.dynamic_index_in_dim(piece, n_hi - 1 - h, 0, keepdims=False)
                mine = mine + lax.ppermute(other, axis, perm_h)
            out.append(mine)
    return jnp.concatenate(out, axis=0)


def shards(hidden_input_state, norm_gain, head_weight, target_ids):
    tokens, local_cols = hidden_input_state.shape
    width, vocab_rows = head_weight.shape
    n_tensor = width // local_cols
    n_outer = lax.psum(1, "outer")
    n_lo = 4 if n_tensor % 4 == 0 else n_tensor
    n_hi = n_tensor // n_lo
    blocks = grid_gather(hidden_input_state.T, "tensor", n_hi, n_lo)
    values_t = blocks.reshape(width, tokens).astype(jnp.float32)
    scaled = lax.rsqrt(jnp.mean(values_t * values_t, axis=0) + epsilon)
    scaled_rows = scaled[:, None]
    normalized_t = values_t * scaled[None, :]
    normed_t = (normalized_t * norm_gain[:, None]).astype(jnp.bfloat16)
    logits = lax.dot_general(
        normed_t, head_weight, (((0,), (0,)), ((), ())), preferred_element_type=jnp.float32
    )
    row_top, row_total = butterfly_softmax_stats(
        jnp.max(logits, axis=1), logits, "tensor", n_tensor
    )
    log_total = row_top + jnp.log(row_total)
    offset = lax.axis_index("tensor") * vocab_rows
    column_ids = offset + lax.broadcasted_iota(jnp.int32, (1, vocab_rows), 1)
    onehot = (column_ids == target_ids[:, None]).astype(jnp.float32)
    dlogits = (jnp.exp(logits - log_total[:, None]) - onehot).astype(jnp.bfloat16)

    core = lax.axis_index("core")
    by_core = normed_t.reshape(n_outer, 2, width // (2 * n_outer), tokens)

    def head_rows(which):
        rows = lax.dynamic_index_in_dim(by_core, which, 1, keepdims=False).reshape(width // 2, tokens)
        return lax.dot_general(
            rows, dlogits, (((1,), (0,)), ((), ())), preferred_element_type=jnp.float32
        )

    sent = lax.ppermute(head_rows(1 - core), "core", [(0, 1), (1, 0)])
    kept = head_rows(core) + sent
    grad_head = lax.psum_scatter(kept, "outer", scatter_dimension=0, tiled=True)

    partial = lax.dot_general(
        head_weight.reshape(n_tensor, local_cols, vocab_rows),
        jnp.broadcast_to(dlogits[None], (n_tensor, tokens, vocab_rows)),
        (((2,), (2,)), ((0,), (0,))),
        preferred_element_type=jnp.float32,
    ).reshape(width, tokens)
    inner_part = jnp.sum(partial * (norm_gain[:, None] * normalized_t), axis=0)
    gain_part = jnp.sum(partial * normalized_t, axis=1)

    gain_rows = -(-local_cols // tokens)
    gain_chunks = jnp.pad(
        gain_part.reshape(n_tensor, local_cols), ((0, 0), (0, gain_rows * tokens - local_cols))
    ).reshape(n_tensor, gain_rows, tokens)
    extra = jnp.concatenate(
        [
            jnp.broadcast_to(inner_part[None, None, :], (n_tensor, 1, tokens)),
            gain_chunks,
            jnp.zeros((n_tensor, 7 - gain_rows, tokens), jnp.float32),
        ],
        axis=1,
    )
    chunks = jnp.concatenate([partial.reshape(n_tensor, local_cols, tokens), extra], axis=1)
    summed = two_stage_reduce_scatter(
        chunks.reshape(n_hi, n_lo, local_cols + 8, tokens), "tensor", n_hi, n_lo
    )
    grad_cols = summed[:local_cols]
    row_inner_sum = summed[local_cols] / width
    gain_local = summed[local_cols + 1 : local_cols + 1 + gain_rows].reshape(-1)[:local_cols]

    normed_gradient = grad_cols.T
    start_col = lax.axis_index("tensor") * local_cols
    normalized_slice = hidden_input_state.astype(jnp.float32) * scaled_rows
    gain_slice = lax.dynamic_slice_in_dim(norm_gain, start_col, local_cols)
    weighted_rows = normed_gradient * gain_slice[None, :]
    hidden_state_gradient = scaled_rows * (
        weighted_rows - normalized_slice * row_inner_sum[:, None]
    )
    norm_gain_gradient = butterfly_sum(butterfly_sum(gain_local, "outer", n_outer), "core", 2)
    return (hidden_state_gradient, grad_head, norm_gain_gradient)


def solution(mesh):
    n_dp, n_tensor = mesh.devices.shape
    split = Mesh(mesh.devices.reshape(n_dp // 2, 2, n_tensor), ("outer", "core", "tensor"))
    dp = ("outer", "core")
    return jax.shard_map(
        shards,
        mesh=split,
        in_specs=(P(dp, "tensor"), P(), P(None, "tensor"), P(dp)),
        out_specs=(P(dp, "tensor"), P(dp, "tensor"), P("tensor")),
        check_vma=False,
    )
```
